512 devices in a mesh: row: 4 (over y_hi), col: 16 (over y_lo, x, core), depth: 8 (over z).
Axes of the slice: x: 4, y: 8 (y_hi: 4, y_lo: 2; y = y_hi * 2 + y_lo), z: 8, core: 2. Of those that a mesh axis runs over, the one named last changes fastest.
Arguments:
- block_values: bfloat16 [32, 16, 16, 128, 128], P(('row', 'depth'), 'col'), may hold values from 0.0049743652 to 0.5
- block_cols: int32 [32, 16, 16], P(('row', 'depth'), 'col'), may hold values from 0 to 511, as said below
- live_count: int32 [32, 16], P(('row', 'depth'), 'col'), may hold values from 8 to 16, as said below
- out_pattern: int32 [4, 16, 32, 2], P('row', 'col'), may hold values from 0 to 511, as said below
Outputs:
- squared_log: bfloat16 [4, 16, 32, 128, 128], P('row', 'col', 'depth')
The draws below stay inside these ranges and needn't reach their ends.
Inputs may be any that keep to these rules, and one draw needn't show every extreme that they name: Block row i's blocks are its first live_count slots; in every draw some block row is full. `block_cols`: the slots of one block row name distinct block columns. Call (k // 16) % 8 the depth part of a block index k and k // 32 its column group. Among the live slots of one block row at most 2 name a column in any one depth part and at most 2 in any one column group; both bounds are reached in every draw. The 32 entries of out_pattern[r, c] are distinct pairs (i, j) with i // 128 == r and j // 32 == c.
All inputs are finite; a program needn't handle non-finite values.
Results may differ from the reference program's by a relative error of at most 0.001.
Values may be sent and summed in bfloat16 or wider, within the bound.
No kernel may reach another device: no remote copies, remote signals or barrier semaphores. Data moves between devices by JAX's collectives and lax.ppermute only.
A program may use at most 128 MiB of HBM per device.

```python
import math
import jax
import jax.numpy as jnp
from jax import lax

BS = 128
NZR = 16
GROUPS = 32
GR = 16
NB = 512
RB = 128
CB = 32
CPAT = 32
N_ROW = 4
N_COL = 16


def structure(key):
    start = jax.random.randint(jax.random.fold_in(key, 101), (NB,), 0, GROUPS)
    shift = jax.random.randint(jax.random.fold_in(key, 102), (NB, GROUPS), 0, GR)
    level = jax.random.randint(jax.random.fold_in(key, 103), (NB,), 0, 2)
    full_row = jax.random.randint(jax.random.fold_in(key, 104), (), 0, NB)
    position = start[:, None] + jnp.arange(NZR, dtype=jnp.int32)[None, :]
    block_ids = position % GROUPS
    wraps = position // GROUPS
    offsets = (jnp.take_along_axis(shift, block_ids, axis=1) + wraps) % GR
    col_ids = block_ids * GR + offsets
    live_rows = jnp.right_shift(jnp.full((NB,), NZR, jnp.int32), level.astype(jnp.int32))
    live_rows = jnp.where(jnp.arange(NB) == full_row, NZR, live_rows)
    return (col_ids.astype(jnp.int32), live_rows.astype(jnp.int32))


def shuffle_one(sub_key):
    return jax.random.permutation(sub_key, RB * CB).astype(jnp.int32)


def pattern_from(key, col_ids, live_rows):
    is_live = jnp.arange(NZR, dtype=jnp.int32)[None, :] < live_rows[:, None]
    second_cols = col_ids[col_ids]
    usable = is_live[:, :, None] & is_live[col_ids]
    row_ids = jnp.broadcast_to(jnp.arange(NB, dtype=jnp.int32)[:, None, None], second_cols.shape)
    reached = jnp.zeros((NB, NB), jnp.int32).at[row_ids.reshape(-1), second_cols.reshape(-1)].max(usable.reshape(-1).astype(jnp.int32))
    row_groups = NB // RB
    col_groups = NB // CB
    cell_marks = reached.reshape(row_groups, RB, col_groups, CB).transpose(0, 2, 1, 3).reshape(row_groups * col_groups, RB * CB)
    group_keys = jax.random.split(jax.random.fold_in(key, 105), row_groups * col_groups)
    shuffled = jax.vmap(shuffle_one)(group_keys)
    scores = cell_marks * (RB * CB) + shuffled
    _, picked = lax.top_k(scores, CPAT)
    group_ids = jnp.arange(row_groups * col_groups, dtype=jnp.int32)
    pick_rows = (group_ids // col_groups)[:, None] * RB + picked // CB
    pick_cols = (group_ids % col_groups)[:, None] * CB + picked % CB
    stacked = jnp.stack([pick_rows, pick_cols], axis=-1)
    return stacked.reshape(row_groups, col_groups, CPAT, 2).astype(jnp.int32)


def draw_block_cols(key, part):
    col_ids, live_rows = structure(key)
    return col_ids.reshape(GROUPS, GR, NZR)


def draw_live_count(key, part):
    col_ids, live_rows = structure(key)
    return live_rows.reshape(GROUPS, GR)


def draw_out_pattern(key, part):
    col_ids, live_rows = structure(key)
    return pattern_from(key, col_ids, live_rows)


def shard_levels(own_key, dims, cuts, low, top_value):
    factor_of, own = 1.0, jax.random.fold_in(own_key, 6)
    for axis_at, parts in cuts:
        heights = jnp.exp(jax.random.uniform(jax.random.fold_in(own, axis_at), (parts,), jnp.float32, low / len(cuts), top_value / len(cuts)))
        factor_of = factor_of * jnp.repeat(heights, dims[axis_at] // parts).reshape([-1 if axis == axis_at else 1 for axis in range(len(dims))])
    return factor_of


def setup_inputs(seed: int = 0) -> dict:
    key_of = jax.random.split(jax.random.key(seed), 5)
    return {
        "block_values": jnp.clip(jnp.exp(math.log(0.5) - 4.61031033 * jax.random.uniform(key_of[0], (GROUPS, GR, NZR, BS, BS), jnp.float32) ** shard_levels(key_of[0], (GROUPS, GR, NZR, BS, BS), ((0, 32), (1, 16)), -0.2, 0.2)), 0.0049743652, 0.5).astype(jnp.bfloat16),
        "block_cols": draw_block_cols(jax.random.fold_in(key_of[4], 71), 0),
        "live_count": draw_live_count(jax.random.fold_in(key_of[4], 71), 0),
        "out_pattern": draw_out_pattern(jax.random.fold_in(key_of[4], 71), 0),
    }


def reference(block_values, block_cols, live_count, out_pattern):
    values = block_values.reshape(NB, NZR, BS, BS)
    col_ids = block_cols.reshape(NB, NZR)
    is_live = jnp.arange(NZR, dtype=jnp.int32)[None, :] < live_count.reshape(NB, 1)
    entries = out_pattern.reshape(-1, 2).astype(jnp.int32)

    def one_block(entry):
        row_pick = entry[0]
        col_pick = entry[1]
        left_blocks = values[row_pick].astype(jnp.float32)
        inner = col_ids[row_pick]
        right_blocks = values[inner].astype(jnp.float32)
        weight = (is_live[row_pick][:, None] & is_live[inner] & (col_ids[inner] == col_pick)).astype(jnp.float32)
        chosen = jnp.einsum("st,stab->sab", weight, right_blocks, precision=lax.Precision.HIGHEST)
        return jnp.einsum("sab,sbc->ac", left_blocks, chosen, precision=lax.Precision.HIGHEST)

    blocks = lax.map(one_block, entries)
    result = jnp.log1p(blocks).astype(jnp.bfloat16)
    return result.reshape(N_ROW, N_COL, CPAT, BS, BS)
```

```python
import math

import jax
import jax.numpy as jnp
from jax import lax
from jax.sharding import PartitionSpec as P


def pack_slots(values, col_ids, targets, is_live, part_count, capacity):
    row_count = col_ids.shape[0]
    block_size = values.shape[-1]
    chosen = (
        targets[:, :, None] == jnp.arange(part_count, dtype=jnp.int32)[None, None, :]
    ) & is_live[:, :, None]
    running = jnp.cumsum(chosen.astype(jnp.int32), axis=1) - 1
    order_in = jnp.sum(jnp.where(chosen, running, 0), axis=2)
    row_ids = jnp.arange(row_count, dtype=jnp.int32)[:, None]
    total = part_count * row_count * capacity
    position = (targets * row_count + row_ids) * capacity + order_in
    position = jnp.where(is_live, position, total).reshape(-1)
    packed = jnp.zeros((total, block_size, block_size), values.dtype)
    packed = packed.at[position].set(values.reshape(-1, block_size, block_size), mode="drop")
    packed_cols = (
        jnp.full((total,), -1, jnp.int32).at[position].set(col_ids.reshape(-1), mode="drop")
    )
    return (
        packed.reshape(part_count, row_count, capacity, block_size, block_size),
        packed_cols.reshape(part_count, row_count, capacity),
    )


def body(block_values, block_cols, live_count, out_pattern):
    depths = lax.axis_size("depth")
    columns = lax.axis_size("col")
    row_groups = lax.axis_size("row")
    row_index = lax.axis_index("row")
    rows_dev = block_values.shape[1]
    slot_count = block_values.shape[2]
    block_size = block_values.shape[3]
    group_rows = columns * rows_dev
    group_count = row_groups * depths
    total_rows = group_count * group_rows
    col_block = total_rows // columns
    pair_size = group_count // columns
    cap_left = slot_count // depths
    cap_right = pair_size * (slot_count // group_count) + min(pair_size, slot_count % group_count)
    values = block_values.reshape(rows_dev, slot_count, block_size, block_size)
    col_ids = block_cols.reshape(rows_dev, slot_count)
    counts = live_count.reshape(rows_dev)
    is_live = jnp.arange(slot_count, dtype=jnp.int32)[None, :] < counts[:, None]
    left_vals, left_cols = pack_slots(
        values, col_ids, col_ids // group_rows % depths, is_live, depths, cap_left
    )
    left_vals, left_cols = (
        lax.all_to_all(left_vals, "depth", split_axis=0, concat_axis=0, tiled=True),
        lax.all_to_all(left_cols, "depth", split_axis=0, concat_axis=0, tiled=True),
    )
    left_vals, left_cols = (
        lax.all_gather(left_vals[None], "col", axis=0, tiled=True),
        lax.all_gather(left_cols[None], "col", axis=0, tiled=True),
    )
    left_shape = left_cols.shape
    source_col = lax.broadcasted_iota(jnp.int32, left_shape, 0)
    source_depth = lax.broadcasted_iota(jnp.int32, left_shape, 1)
    source_row = lax.broadcasted_iota(jnp.int32, left_shape, 2)
    left_rows = (
        (row_index * depths + source_depth) * group_rows + source_col * rows_dev + source_row
    ).reshape(-1)
    left_flat = left_vals.reshape(-1, block_size, block_size)
    left_ids = left_cols.reshape(-1)
    right_vals, right_cols = pack_slots(
        values, col_ids, col_ids // col_block, is_live, columns, cap_right
    )
    right_vals, right_cols = (
        lax.all_to_all(right_vals, "col", split_axis=0, concat_axis=0, tiled=True),
        lax.all_to_all(right_cols, "col", split_axis=0, concat_axis=0, tiled=True),
    )
    right_vals, right_cols = (
        lax.all_gather(right_vals[None], "row", axis=0, tiled=True),
        lax.all_gather(right_cols[None], "row", axis=0, tiled=True),
    )
    right_flat = right_vals.reshape(-1, cap_right, block_size, block_size)
    right_ids = right_cols.reshape(-1, cap_right)
    pattern_rows = out_pattern[0, 0, :, 0]
    pattern_cols = out_pattern[0, 0, :, 1]
    local_row = pattern_rows - row_index * (depths * group_rows)
    left_pos = (local_row % group_rows) * depths + local_row // group_rows
    left_sel = left_pos[:, None] * cap_left + jnp.arange(cap_left, dtype=jnp.int32)[None, :]
    left_flat = left_vals.reshape(-1, block_size, block_size)
    left_ids = left_cols.reshape(-1)
    left_pick = jnp.take(left_flat, left_sel.reshape(-1), axis=0)
    inner = jnp.take(left_ids, left_sel, axis=0)
    safe_inner = jnp.maximum(inner, 0)
    right_row = safe_inner // (depths * group_rows) * columns + safe_inner % group_rows
    right_ids = right_cols.reshape(-1, cap_right)
    right_flat = right_vals.reshape(-1, block_size, block_size)
    right_here = jnp.take(right_ids, right_row, axis=0)
    matched = (right_here == pattern_cols[:, None, None]) & (inner >= 0)[:, :, None]
    slot = jnp.sum(
        jnp.where(matched, jnp.arange(cap_right, dtype=jnp.int32)[None, None, :], 0), axis=2
    )
    found = jnp.any(matched, axis=2)
    right_pick = jnp.take(right_flat, (right_row * cap_right + slot).reshape(-1), axis=0)
    right_pick = jnp.where(
        found.reshape(-1)[:, None, None], right_pick, jnp.zeros_like(right_pick)
    )
    pattern_len = pattern_rows.shape[0]
    left_pick = left_pick.reshape(pattern_len, cap_left, block_size, block_size)
    right_pick = right_pick.reshape(pattern_len, cap_left, block_size, block_size)
    partial_sum = jnp.einsum(
        "pqab,pqbc->pac", left_pick, right_pick, preferred_element_type=jnp.float32
    )
    share = lax.psum_scatter(partial_sum[None, None], "depth", scatter_dimension=2, tiled=True)
    return jnp.log1p(share).astype(jnp.bfloat16)


def solution(mesh):
    in_specs = (
        P(("row", "depth"), "col", None, None, None),
        P(("row", "depth"), "col", None),
        P(("row", "depth"), "col"),
        P("row", "col", None, None),
    )
    out_specs = P("row", "col", "depth", None, None)
    return jax.shard_map(body, mesh=mesh, in_specs=in_specs, out_specs=out_specs, check_vma=False)
```

```python
import jax
import jax.numpy as jnp
from jax import lax
from jax.sharding import PartitionSpec as P


def pack_slots(values, col_ids, targets, is_live, part_count, capacity):
    row_count = col_ids.shape[0]
    block_size = values.shape[-1]
    chosen = (
        targets[:, :, None] == jnp.arange(part_count, dtype=jnp.int32)[None, None, :]
    ) & is_live[:, :, None]
    running = jnp.cumsum(chosen.astype(jnp.int32), axis=1) - 1
    order_in = jnp.sum(jnp.where(chosen, running, 0), axis=2)
    row_ids = jnp.arange(row_count, dtype=jnp.int32)[:, None]
    total = part_count * row_count * capacity
    position = (targets * row_count + row_ids) * capacity + order_in
    position = jnp.where(is_live, position, total).reshape(-1)
    packed = jnp.zeros((total, block_size, block_size), values.dtype)
    packed = packed.at[position].set(values.reshape(-1, block_size, block_size), mode="drop")
    return packed.reshape(part_count, row_count, capacity, block_size, block_size)


def body(block_values, block_cols, live_count, out_pattern):
    depths = lax.axis_size("depth")
    columns = lax.axis_size("col")
    row_groups = lax.axis_size("row")
    row_index = lax.axis_index("row")
    depth_index = lax.axis_index("depth")
    col_index = lax.axis_index("col")
    slot_count = block_values.shape[2]
    block_size = block_values.shape[3]
    group_rows = columns
    plane_rows = depths * group_rows
    col_block = row_groups * plane_rows // columns
    cap_left = slot_count // depths
    cap_right = 2
    values = block_values.reshape(1, slot_count, block_size, block_size)
    col_ids = block_cols.reshape(1, slot_count)
    counts = live_count.reshape(1)
    slots = jnp.arange(slot_count, dtype=jnp.int32)
    is_live = slots[None, :] < counts[:, None]

    meta = jnp.concatenate([col_ids, counts[:, None]], axis=1).astype(jnp.float32)
    meta = lax.all_gather(meta, ("row", "depth", "col"), axis=0, tiled=True).astype(jnp.int32)
    all_cols = meta[:, :slot_count]
    all_live = slots[None, :] < meta[:, slot_count:]

    left_vals = pack_slots(
        values, col_ids, col_ids // group_rows % depths, is_live, depths, cap_left
    )
    left_vals = lax.all_to_all(left_vals, "depth", split_axis=0, concat_axis=0, tiled=True)
    left_vals = lax.all_gather(left_vals[None], "col", axis=0, tiled=True)
    right_vals = pack_slots(
        values, col_ids, col_ids // col_block, is_live, columns, cap_right
    )
    right_vals = lax.all_to_all(right_vals, "col", split_axis=0, concat_axis=0, tiled=True)
    right_parts = [right_vals]
    for shift in range(1, row_groups):
        right_parts.append(
            lax.ppermute(
                right_vals,
                "row",
                perm=[(src, (src + shift) % row_groups) for src in range(row_groups)],
            )
        )
    right_flat = jnp.stack(right_parts).reshape(-1, block_size, block_size)

    pattern_rows = out_pattern[0, 0, :, 0]
    pattern_cols = out_pattern[0, 0, :, 1]
    pattern_len = pattern_rows.shape[0]
    local_row = pattern_rows - row_index * plane_rows
    left_pos = (local_row % group_rows) * depths + local_row // group_rows
    left_sel = left_pos[:, None] * cap_left + jnp.arange(cap_left, dtype=jnp.int32)[None, :]

    row_cols = jnp.take(all_cols, pattern_rows, axis=0)
    row_live = jnp.take(all_live, pattern_rows, axis=0)
    chosen = row_live & (row_cols // group_rows % depths == depth_index)
    rank = jnp.cumsum(chosen.astype(jnp.int32), axis=1) - 1
    picks = jnp.arange(cap_left, dtype=jnp.int32)
    hit = chosen[:, None, :] & (rank[:, None, :] == picks[None, :, None])
    has_inner = jnp.any(hit, axis=2)
    inner = jnp.sum(jnp.where(hit, row_cols[:, None, :], 0), axis=2)

    inner_cols = jnp.take(all_cols, inner, axis=0)
    inner_live = jnp.take(all_live, inner, axis=0)
    in_group = inner_live & (inner_cols // col_block == col_index)
    before = jnp.cumsum(in_group.astype(jnp.int32), axis=2) - 1
    match = in_group & (inner_cols == pattern_cols[:, None, None])
    found = jnp.any(match, axis=2) & has_inner
    slot = jnp.sum(jnp.where(match, before, 0), axis=2)
    shift_of = (row_index - inner // plane_rows) % row_groups
    right_row = shift_of * columns + inner % group_rows

    left_flat = left_vals.reshape(-1, block_size, block_size)
    left_pick = jnp.take(left_flat, left_sel.reshape(-1), axis=0)
    right_pick = jnp.take(right_flat, (right_row * cap_right + slot).reshape(-1), axis=0)
    right_pick = jnp.where(
        found.reshape(-1)[:, None, None], right_pick, jnp.zeros_like(right_pick)
    )
    left_pick = left_pick.reshape(pattern_len, cap_left, block_size, block_size)
    right_pick = right_pick.reshape(pattern_len, cap_left, block_size, block_size)
    partial_sum = jnp.einsum(
        "pqab,pqbc->pac", left_pick, right_pick, preferred_element_type=jnp.float32
    )
    share = lax.psum_scatter(partial_sum[None, None], "depth", scatter_dimension=2, tiled=True)
    return jnp.log1p(share).astype(jnp.bfloat16)


def solution(mesh):
    in_specs = (
        P(("row", "depth"), "col", None, None, None),
        P(("row", "depth"), "col", None),
        P(("row", "depth"), "col"),
        P("row", "col", None, None),
    )
    out_specs = P("row", "col", "depth", None, None)
    return jax.shard_map(body, mesh=mesh, in_specs=in_specs, out_specs=out_specs, check_vma=False)
```

```python
import math

import jax
import jax.numpy as jnp
from jax import lax
from jax.sharding import PartitionSpec as P


def pack_slots(values, col_ids, targets, is_live, part_count, capacity):
    row_count = col_ids.shape[0]
    block_size = values.shape[-1]
    chosen = (
        targets[:, :, None] == jnp.arange(part_count, dtype=jnp.int32)[None, None, :]
    ) & is_live[:, :, None]
    running = jnp.cumsum(chosen.astype(jnp.int32), axis=1) - 1
    order_in = jnp.sum(jnp.where(chosen, running, 0), axis=2)
    row_ids = jnp.arange(row_count, dtype=jnp.int32)[:, None]
    total = part_count * row_count * capacity
    position = (targets * row_count + row_ids) * capacity + order_in
    position = jnp.where(is_live, position, total).reshape(-1)
    packed = jnp.zeros((total, block_size, block_size), values.dtype)
    packed = packed.at[position].set(values.reshape(-1, block_size, block_size), mode="drop")
    packed_cols = (
        jnp.full((total,), -1, jnp.int32).at[position].set(col_ids.reshape(-1), mode="drop")
    )
    return (
        packed.reshape(part_count, row_count, capacity, block_size, block_size),
        packed_cols.reshape(part_count, row_count, capacity),
    )


def body(block_values, block_cols, live_count, out_pattern):
    depths = lax.axis_size("depth")
    columns = lax.axis_size("col")
    row_groups = lax.axis_size("row")
    row_index = lax.axis_index("row")
    rows_dev = block_values.shape[1]
    slot_count = block_values.shape[2]
    block_size = block_values.shape[3]
    group_rows = columns * rows_dev
    group_count = row_groups * depths
    total_rows = group_count * group_rows
    col_block = total_rows // columns
    pair_size = group_count // columns
    cap_left = slot_count // depths
    cap_right = pair_size * (slot_count // group_count) + min(pair_size, slot_count % group_count)
    values = block_values.reshape(rows_dev, slot_count, block_size, block_size)
    col_ids = block_cols.reshape(rows_dev, slot_count)
    counts = live_count.reshape(rows_dev)
    is_live = jnp.arange(slot_count, dtype=jnp.int32)[None, :] < counts[:, None]
    left_vals, left_cols = pack_slots(
        values, col_ids, col_ids // group_rows % depths, is_live, depths, cap_left
    )
    left_vals, left_cols = (
        lax.all_to_all(left_vals, "depth", split_axis=0, concat_axis=0, tiled=True),
        lax.all_to_all(left_cols, "depth", split_axis=0, concat_axis=0, tiled=True),
    )
    left_vals, left_cols = (
        lax.all_gather(left_vals[None], "col", axis=0, tiled=True),
        lax.all_gather(left_cols[None], "col", axis=0, tiled=True),
    )
    left_shape = left_cols.shape
    source_col = lax.broadcasted_iota(jnp.int32, left_shape, 0)
    source_depth = lax.broadcasted_iota(jnp.int32, left_shape, 1)
    source_row = lax.broadcasted_iota(jnp.int32, left_shape, 2)
    left_rows = (
        (row_index * depths + source_depth) * group_rows + source_col * rows_dev + source_row
    ).reshape(-1)
    left_flat = left_vals.reshape(-1, block_size, block_size)
    left_ids = left_cols.reshape(-1)
    right_vals, right_cols = pack_slots(
        values, col_ids, col_ids // col_block, is_live, columns, cap_right
    )
    right_vals, right_cols = (
        lax.all_to_all(right_vals, "col", split_axis=0, concat_axis=0, tiled=True),
        lax.all_to_all(right_cols, "col", split_axis=0, concat_axis=0, tiled=True),
    )
    row_perms = [
        [(src, (src + shift) % row_groups) for src in range(row_groups)]
        for shift in range(1, row_groups)
    ]
    right_vals = jnp.stack(
        [right_vals] + [lax.ppermute(right_vals, "row", perm=perm) for perm in row_perms]
    )
    right_cols = jnp.stack(
        [right_cols] + [lax.ppermute(right_cols, "row", perm=perm) for perm in row_perms]
    )
    pattern_rows = out_pattern[0, 0, :, 0]
    pattern_cols = out_pattern[0, 0, :, 1]
    local_row = pattern_rows - row_index * (depths * group_rows)
    left_pos = (local_row % group_rows) * depths + local_row // group_rows
    left_sel = left_pos[:, None] * cap_left + jnp.arange(cap_left, dtype=jnp.int32)[None, :]
    left_flat = left_vals.reshape(-1, block_size, block_size)
    left_ids = left_cols.reshape(-1)
    left_pick = jnp.take(left_flat, left_sel.reshape(-1), axis=0)
    inner = jnp.take(left_ids, left_sel, axis=0)
    safe_inner = jnp.maximum(inner, 0)
    right_row = (row_index - safe_inner // (depths * group_rows)) % row_groups * columns + safe_inner % group_rows
    right_ids = right_cols.reshape(-1, cap_right)
    right_flat = right_vals.reshape(-1, block_size, block_size)
    right_here = jnp.take(right_ids, right_row, axis=0)
    matched = (right_here == pattern_cols[:, None, None]) & (inner >= 0)[:, :, None]
    slot = jnp.sum(
        jnp.where(matched, jnp.arange(cap_right, dtype=jnp.int32)[None, None, :], 0), axis=2
    )
    found = jnp.any(matched, axis=2)
    right_pick = jnp.take(right_flat, (right_row * cap_right + slot).reshape(-1), axis=0)
    right_pick = jnp.where(
        found.reshape(-1)[:, None, None], right_pick, jnp.zeros_like(right_pick)
    )
    pattern_len = pattern_rows.shape[0]
    left_pick = left_pick.reshape(pattern_len, cap_left, block_size, block_size)
    right_pick = right_pick.reshape(pattern_len, cap_left, block_size, block_size)
    partial_sum = jnp.einsum(
        "pqab,pqbc->pac", left_pick, right_pick, preferred_element_type=jnp.float32
    )
    share = lax.psum_scatter(partial_sum[None, None], "depth", scatter_dimension=2, tiled=True)
    return jnp.log1p(share).astype(jnp.bfloat16)


def solution(mesh):
    in_specs = (
        P(("row", "depth"), "col", None, None, None),
        P(("row", "depth"), "col", None),
        P(("row", "depth"), "col"),
        P("row", "col", None, None),
    )
    out_specs = P("row", "col", "depth", None, None)
    return jax.shard_map(body, mesh=mesh, in_specs=in_specs, out_specs=out_specs, check_vma=False)
```

```python
import math

import jax
import jax.numpy as jnp
from jax import lax
from jax.sharding import Mesh, PartitionSpec as P

COL = ("ylo", "x", "core")


def pack_slots(values, col_ids, targets, is_live, part_count, capacity):
    row_count = col_ids.shape[0]
    block_size = values.shape[-1]
    chosen = (
        targets[:, :, None] == jnp.arange(part_count, dtype=jnp.int32)[None, None, :]
    ) & is_live[:, :, None]
    running = jnp.cumsum(chosen.astype(jnp.int32), axis=1) - 1
    order_in = jnp.sum(jnp.where(chosen, running, 0), axis=2)
    row_ids = jnp.arange(row_count, dtype=jnp.int32)[:, None]
    total = part_count * row_count * capacity
    position = (targets * row_count + row_ids) * capacity + order_in
    position = jnp.where(is_live, position, total).reshape(-1)
    packed = jnp.zeros((total, block_size, block_size), values.dtype)
    packed = packed.at[position].set(values.reshape(-1, block_size, block_size), mode="drop")
    packed_cols = (
        jnp.full((total,), -1, jnp.int32).at[position].set(col_ids.reshape(-1), mode="drop")
    )
    return (
        packed.reshape(part_count, row_count, capacity, block_size, block_size),
        packed_cols.reshape(part_count, row_count, capacity),
    )


def body(block_values, block_cols, live_count, out_pattern):
    depths = lax.axis_size("depth")
    columns = lax.axis_size(COL)
    row_groups = lax.axis_size("row")
    row_index = lax.axis_index("row")
    rows_dev = block_values.shape[1]
    slot_count = block_values.shape[2]
    block_size = block_values.shape[3]
    group_rows = columns * rows_dev
    group_count = row_groups * depths
    total_rows = group_count * group_rows
    col_block = total_rows // columns
    pair_size = group_count // columns
    cap_left = slot_count // depths
    cap_right = pair_size * (slot_count // group_count) + min(pair_size, slot_count % group_count)
    values = block_values.reshape(rows_dev, slot_count, block_size, block_size)
    col_ids = block_cols.reshape(rows_dev, slot_count)
    counts = live_count.reshape(rows_dev)
    is_live = jnp.arange(slot_count, dtype=jnp.int32)[None, :] < counts[:, None]
    left_vals, left_cols = pack_slots(
        values, col_ids, col_ids // group_rows % depths, is_live, depths, cap_left
    )
    left_vals, left_cols = (
        lax.all_to_all(left_vals, "depth", split_axis=0, concat_axis=0, tiled=True),
        lax.all_to_all(left_cols, "depth", split_axis=0, concat_axis=0, tiled=True),
    )
    chip_vals = lax.all_gather(left_vals[None], ("ylo", "x"), axis=0, tiled=True)
    other_vals = lax.ppermute(chip_vals, "core", perm=[(0, 1), (1, 0)])
    core_index = lax.axis_index("core")
    core_count = lax.axis_size("core")
    left_cols = lax.all_gather(left_cols[None], COL, axis=0, tiled=True)
    right_vals, right_cols = pack_slots(
        values, col_ids, col_ids // col_block, is_live, columns, cap_right
    )
    right_vals, right_cols = (
        lax.all_to_all(right_vals, COL, split_axis=0, concat_axis=0, tiled=True),
        lax.all_to_all(right_cols, COL, split_axis=0, concat_axis=0, tiled=True),
    )
    right_vals, right_cols = (
        lax.all_gather(right_vals[None], "row", axis=0, tiled=True),
        lax.all_gather(right_cols[None], "row", axis=0, tiled=True),
    )
    right_flat = right_vals.reshape(-1, cap_right, block_size, block_size)
    right_ids = right_cols.reshape(-1, cap_right)
    pattern_rows = out_pattern[0, 0, :, 0]
    pattern_cols = out_pattern[0, 0, :, 1]
    local_row = pattern_rows - row_index * (depths * group_rows)
    left_pos = (local_row % group_rows) * depths + local_row // group_rows
    left_sel = left_pos[:, None] * cap_left + jnp.arange(cap_left, dtype=jnp.int32)[None, :]
    left_ids = left_cols.reshape(-1)
    source_col = local_row % group_rows
    chip_sel = (
        (source_col // core_count * depths + local_row // group_rows)[:, None] * cap_left
        + jnp.arange(cap_left, dtype=jnp.int32)[None, :]
    ).reshape(-1)
    own_core = jnp.repeat(source_col % core_count == core_index, cap_left)
    left_pick = jnp.where(
        own_core[:, None, None],
        jnp.take(chip_vals.reshape(-1, block_size, block_size), chip_sel, axis=0),
        jnp.take(other_vals.reshape(-1, block_size, block_size), chip_sel, axis=0),
    )
    inner = jnp.take(left_ids, left_sel, axis=0)
    safe_inner = jnp.maximum(inner, 0)
    right_row = safe_inner // (depths * group_rows) * columns + safe_inner % group_rows
    right_ids = right_cols.reshape(-1, cap_right)
    right_flat = right_vals.reshape(-1, block_size, block_size)
    right_here = jnp.take(right_ids, right_row, axis=0)
    matched = (right_here == pattern_cols[:, None, None]) & (inner >= 0)[:, :, None]
    slot = jnp.sum(
        jnp.where(matched, jnp.arange(cap_right, dtype=jnp.int32)[None, None, :], 0), axis=2
    )
    found = jnp.any(matched, axis=2)
    right_pick = jnp.take(right_flat, (right_row * cap_right + slot).reshape(-1), axis=0)
    right_pick = jnp.where(
        found.reshape(-1)[:, None, None], right_pick, jnp.zeros_like(right_pick)
    )
    pattern_len = pattern_rows.shape[0]
    left_pick = left_pick.reshape(pattern_len, cap_left, block_size, block_size)
    right_pick = right_pick.reshape(pattern_len, cap_left, block_size, block_size)
    partial_sum = jnp.einsum(
        "pqab,pqbc->pac", left_pick, right_pick, preferred_element_type=jnp.float32
    )
    share = lax.psum_scatter(partial_sum[None, None], "depth", scatter_dimension=2, tiled=True)
    return jnp.log1p(share).astype(jnp.bfloat16)


def solution(mesh):
    rows, cols, depths = mesh.devices.shape
    chips_x = cols // 4
    fine = Mesh(
        mesh.devices.reshape(rows, 2, chips_x, 2, depths), ("row", "ylo", "x", "core", "depth")
    )
    in_specs = (
        P(("row", "depth"), COL, None, None, None),
        P(("row", "depth"), COL, None),
        P(("row", "depth"), COL),
        P("row", COL, None, None),
    )
    out_specs = P("row", COL, "depth", None, None)
    return jax.shard_map(body, mesh=fine, in_specs=in_specs, out_specs=out_specs, check_vma=False)
```

```python
import math

import jax
import jax.numpy as jnp
from jax import lax
from jax.sharding import PartitionSpec as P


def pack_slots(values, col_ids, targets, is_live, part_count, capacity):
    row_count = col_ids.shape[0]
    block_size = values.shape[-1]
    chosen = (
        targets[:, :, None] == jnp.arange(part_count, dtype=jnp.int32)[None, None, :]
    ) & is_live[:, :, None]
    running = jnp.cumsum(chosen.astype(jnp.int32), axis=1) - 1
    order_in = jnp.sum(jnp.where(chosen, running, 0), axis=2)
    row_ids = jnp.arange(row_count, dtype=jnp.int32)[:, None]
    total = part_count * row_count * capacity
    position = (targets * row_count + row_ids) * capacity + order_in
    position = jnp.where(is_live, position, total).reshape(-1)
    packed = jnp.zeros((total, block_size, block_size), values.dtype)
    packed = packed.at[position].set(values.reshape(-1, block_size, block_size), mode="drop")
    packed_cols = (
        jnp.full((total,), -1, jnp.int32).at[position].set(col_ids.reshape(-1), mode="drop")
    )
    return (
        packed.reshape(part_count, row_count, capacity, block_size, block_size),
        packed_cols.reshape(part_count, row_count, capacity),
    )


def gather_by_exchange(x, axis, size):
    copies = jnp.broadcast_to(x[None], (size,) + x.shape)
    return lax.all_to_all(copies, axis, split_axis=0, concat_axis=0, tiled=True)


def body(block_values, block_cols, live_count, out_pattern):
    depths = lax.axis_size("depth")
    columns = lax.axis_size("col")
    row_groups = lax.axis_size("row")
    row_index = lax.axis_index("row")
    rows_dev = block_values.shape[1]
    slot_count = block_values.shape[2]
    block_size = block_values.shape[3]
    group_rows = columns * rows_dev
    group_count = row_groups * depths
    total_rows = group_count * group_rows
    col_block = total_rows // columns
    pair_size = group_count // columns
    cap_left = slot_count // depths
    cap_right = pair_size * (slot_count // group_count) + min(pair_size, slot_count % group_count)
    values = block_values.reshape(rows_dev, slot_count, block_size, block_size)
    col_ids = block_cols.reshape(rows_dev, slot_count)
    counts = live_count.reshape(rows_dev)
    is_live = jnp.arange(slot_count, dtype=jnp.int32)[None, :] < counts[:, None]
    left_vals, left_cols = pack_slots(
        values, col_ids, col_ids // group_rows % depths, is_live, depths, cap_left
    )
    left_vals, left_cols = (
        lax.all_to_all(left_vals, "depth", split_axis=0, concat_axis=0, tiled=True),
        lax.all_to_all(left_cols, "depth", split_axis=0, concat_axis=0, tiled=True),
    )
    left_vals = lax.all_gather(left_vals[None], "col", axis=0, tiled=True)
    left_cols = gather_by_exchange(left_cols, "col", columns)
    left_shape = left_cols.shape
    source_col = lax.broadcasted_iota(jnp.int32, left_shape, 0)
    source_depth = lax.broadcasted_iota(jnp.int32, left_shape, 1)
    source_row = lax.broadcasted_iota(jnp.int32, left_shape, 2)
    left_rows = (
        (row_index * depths + source_depth) * group_rows + source_col * rows_dev + source_row
    ).reshape(-1)
    left_flat = left_vals.reshape(-1, block_size, block_size)
    left_ids = left_cols.reshape(-1)
    right_vals, right_cols = pack_slots(
        values, col_ids, col_ids // col_block, is_live, columns, cap_right
    )
    right_vals, right_cols = (
        lax.all_to_all(right_vals, "col", split_axis=0, concat_axis=0, tiled=True),
        lax.all_to_all(right_cols, "col", split_axis=0, concat_axis=0, tiled=True),
    )
    right_vals = gather_by_exchange(right_vals, "row", row_groups)
    right_cols = gather_by_exchange(right_cols, "row", row_groups)
    right_flat = right_vals.reshape(-1, cap_right, block_size, block_size)
    right_ids = right_cols.reshape(-1, cap_right)
    pattern_rows = out_pattern[0, 0, :, 0]
    pattern_cols = out_pattern[0, 0, :, 1]
    local_row = pattern_rows - row_index * (depths * group_rows)
    left_pos = (local_row % group_rows) * depths + local_row // group_rows
    left_sel = left_pos[:, None] * cap_left + jnp.arange(cap_left, dtype=jnp.int32)[None, :]
    left_flat = left_vals.reshape(-1, block_size, block_size)
    left_ids = left_cols.reshape(-1)
    left_pick = jnp.take(left_flat, left_sel.reshape(-1), axis=0)
    inner = jnp.take(left_ids, left_sel, axis=0)
    safe_inner = jnp.maximum(inner, 0)
    right_row = safe_inner // (depths * group_rows) * columns + safe_inner % group_rows
    right_ids = right_cols.reshape(-1, cap_right)
    right_flat = right_vals.reshape(-1, block_size, block_size)
    right_here = jnp.take(right_ids, right_row, axis=0)
    matched = (right_here == pattern_cols[:, None, None]) & (inner >= 0)[:, :, None]
    slot = jnp.sum(
        jnp.where(matched, jnp.arange(cap_right, dtype=jnp.int32)[None, None, :], 0), axis=2
    )
    found = jnp.any(matched, axis=2)
    right_pick = jnp.take(right_flat, (right_row * cap_right + slot).reshape(-1), axis=0)
    right_pick = jnp.where(
        found.reshape(-1)[:, None, None], right_pick, jnp.zeros_like(right_pick)
    )
    pattern_len = pattern_rows.shape[0]
    left_pick = left_pick.reshape(pattern_len, cap_left, block_size, block_size)
    right_pick = right_pick.reshape(pattern_len, cap_left, block_size, block_size)
    partial_sum = jnp.einsum(
        "pqab,pqbc->pac", left_pick, right_pick, preferred_element_type=jnp.float32
    )
    share = lax.psum_scatter(partial_sum[None, None], "depth", scatter_dimension=2, tiled=True)
    return jnp.log1p(share).astype(jnp.bfloat16)


def solution(mesh):
    in_specs = (
        P(("row", "depth"), "col", None, None, None),
        P(("row", "depth"), "col", None),
        P(("row", "depth"), "col"),
        P("row", "col", None, None),
    )
    out_specs = P("row", "col", "depth", None, None)
    return jax.shard_map(body, mesh=mesh, in_specs=in_specs, out_specs=out_specs, check_vma=False)
```

```python
import jax
import jax.numpy as jnp
from jax import lax
from jax.sharding import PartitionSpec as P

ID_ROWS = 16
ID_BASE = 32


def pack_slots(values, col_ids, targets, is_live, part_count, capacity):
    slot_count = col_ids.shape[0]
    block_size = values.shape[-1]
    chosen = (targets[:, None] == jnp.arange(part_count, dtype=jnp.int32)[None, :]) & is_live[:, None]
    running = jnp.cumsum(chosen.astype(jnp.int32), axis=0) - 1
    order_in = jnp.sum(jnp.where(chosen, running, 0), axis=1)
    total = part_count * capacity
    position = jnp.where(is_live, targets * capacity + order_in, total)
    packed = jnp.zeros((total, block_size, block_size), values.dtype)
    packed = packed.at[position].set(values, mode="drop")
    packed_cols = jnp.full((total,), -1, jnp.int32).at[position].set(col_ids, mode="drop")
    high = packed_cols // ID_BASE
    low = packed_cols - high * ID_BASE
    codes = jnp.stack([high, low]).reshape(2, part_count, capacity).transpose(1, 0, 2)
    id_rows = jnp.zeros((part_count, ID_ROWS, block_size), values.dtype)
    id_rows = id_rows.at[:, :2, :capacity].set(codes.astype(values.dtype))
    return jnp.concatenate(
        [packed.reshape(part_count, capacity * block_size, block_size), id_rows], axis=1
    )


def unpack_ids(payload, capacity, block_size):
    codes = payload[..., capacity * block_size : capacity * block_size + 2, :capacity]
    codes = codes.astype(jnp.int32)
    return codes[..., 0, :] * ID_BASE + codes[..., 1, :]


def unpack_blocks(payload, capacity, block_size):
    blocks = payload[..., : capacity * block_size, :]
    return blocks.reshape(-1, block_size, block_size)


def gather_by_exchange(x, axis, size):
    copies = jnp.broadcast_to(x[None], (size,) + x.shape)
    return lax.all_to_all(copies, axis, split_axis=0, concat_axis=0, tiled=True)


def body(block_values, block_cols, live_count, out_pattern):
    depths = lax.axis_size("depth")
    columns = lax.axis_size("col")
    row_groups = lax.axis_size("row")
    row_index = lax.axis_index("row")
    slot_count = block_values.shape[2]
    block_size = block_values.shape[3]
    group_rows = columns
    plane_rows = depths * group_rows
    col_block = row_groups * plane_rows // columns
    cap_left = slot_count // depths
    cap_right = 2
    values = block_values.reshape(slot_count, block_size, block_size)
    col_ids = block_cols.reshape(slot_count)
    is_live = jnp.arange(slot_count, dtype=jnp.int32) < live_count.reshape(())

    left = pack_slots(values, col_ids, col_ids // group_rows % depths, is_live, depths, cap_left)
    left = lax.all_to_all(left, "depth", split_axis=0, concat_axis=0, tiled=True)
    left = lax.all_gather(left[None], "col", axis=0, tiled=True)
    right = pack_slots(values, col_ids, col_ids // col_block, is_live, columns, cap_right)
    right = lax.all_to_all(right, "col", split_axis=0, concat_axis=0, tiled=True)
    right = gather_by_exchange(right, "row", row_groups)

    left_ids = unpack_ids(left, cap_left, block_size).reshape(-1)
    right_ids = unpack_ids(right, cap_right, block_size).reshape(-1, cap_right)
    left_flat = unpack_blocks(left, cap_left, block_size)
    right_flat = unpack_blocks(right, cap_right, block_size)

    pattern_rows = out_pattern[0, 0, :, 0]
    pattern_cols = out_pattern[0, 0, :, 1]
    pattern_len = pattern_rows.shape[0]
    local_row = pattern_rows - row_index * plane_rows
    left_pos = (local_row % group_rows) * depths + local_row // group_rows
    left_sel = left_pos[:, None] * cap_left + jnp.arange(cap_left, dtype=jnp.int32)[None, :]
    left_pick = jnp.take(left_flat, left_sel.reshape(-1), axis=0)
    inner = jnp.take(left_ids, left_sel, axis=0)
    safe_inner = jnp.maximum(inner, 0)
    right_row = safe_inner // plane_rows * columns + safe_inner % group_rows
    right_here = jnp.take(right_ids, right_row, axis=0)
    matched = (right_here == pattern_cols[:, None, None]) & (inner >= 0)[:, :, None]
    slot = jnp.sum(
        jnp.where(matched, jnp.arange(cap_right, dtype=jnp.int32)[None, None, :], 0), axis=2
    )
    found = jnp.any(matched, axis=2)
    right_pick = jnp.take(right_flat, (right_row * cap_right + slot).reshape(-1), axis=0)
    right_pick = jnp.where(
        found.reshape(-1)[:, None, None], right_pick, jnp.zeros_like(right_pick)
    )
    left_pick = left_pick.reshape(pattern_len, cap_left, block_size, block_size)
    right_pick = right_pick.reshape(pattern_len, cap_left, block_size, block_size)
    partial_sum = jnp.einsum(
        "pqab,pqbc->pac", left_pick, right_pick, preferred_element_type=jnp.float32
    )
    share = lax.psum_scatter(partial_sum[None, None], "depth", scatter_dimension=2, tiled=True)
    return jnp.log1p(share).astype(jnp.bfloat16)


def solution(mesh):
    in_specs = (
        P(("row", "depth"), "col", None, None, None),
        P(("row", "depth"), "col", None),
        P(("row", "depth"), "col"),
        P("row", "col", None, None),
    )
    out_specs = P("row", "col", "depth", None, None)
    return jax.shard_map(body, mesh=mesh, in_specs=in_specs, out_specs=out_specs, check_vma=False)
```

```python
import math

import jax
import jax.numpy as jnp
from jax import lax
from jax.sharding import PartitionSpec as P


def pack_slots(values, col_ids, targets, is_live, part_count, capacity):
    row_count = col_ids.shape[0]
    block_size = values.shape[-1]
    chosen = (
        targets[:, :, None] == jnp.arange(part_count, dtype=jnp.int32)[None, None, :]
    ) & is_live[:, :, None]
    running = jnp.cumsum(chosen.astype(jnp.int32), axis=1) - 1
    order_in = jnp.sum(jnp.where(chosen, running, 0), axis=2)
    row_ids = jnp.arange(row_count, dtype=jnp.int32)[:, None]
    total = part_count * row_count * capacity
    position = (targets * row_count + row_ids) * capacity + order_in
    position = jnp.where(is_live, position, total).reshape(-1)
    packed = jnp.zeros((total, block_size, block_size), values.dtype)
    packed = packed.at[position].set(values.reshape(-1, block_size, block_size), mode="drop")
    packed_cols = (
        jnp.full((total,), -1, jnp.int32).at[position].set(col_ids.reshape(-1), mode="drop")
    )
    return (
        packed.reshape(part_count, row_count, capacity, block_size, block_size),
        packed_cols.reshape(part_count, row_count, capacity),
    )


def body(block_values, block_cols, live_count, out_pattern):
    depths = lax.axis_size("depth")
    columns = lax.axis_size("col")
    row_groups = lax.axis_size("row")
    row_index = lax.axis_index("row")
    rows_dev = block_values.shape[1]
    slot_count = block_values.shape[2]
    block_size = block_values.shape[3]
    group_rows = columns * rows_dev
    group_count = row_groups * depths
    total_rows = group_count * group_rows
    col_block = total_rows // columns
    pair_size = group_count // columns
    cap_left = slot_count // depths
    cap_right = pair_size * (slot_count // group_count) + min(pair_size, slot_count % group_count)
    values = block_values.reshape(rows_dev, slot_count, block_size, block_size)
    col_ids = block_cols.reshape(rows_dev, slot_count)
    counts = live_count.reshape(rows_dev)
    is_live = jnp.arange(slot_count, dtype=jnp.int32)[None, :] < counts[:, None]
    right_vals, right_cols = pack_slots(
        values, col_ids, col_ids // col_block, is_live, columns, cap_right
    )
    right_vals, right_cols = (
        lax.all_to_all(right_vals, "col", split_axis=0, concat_axis=0, tiled=True),
        lax.all_to_all(right_cols, "col", split_axis=0, concat_axis=0, tiled=True),
    )
    right_rows_vals, right_rows_cols = (
        lax.all_gather(right_vals[None], "row", axis=0, tiled=True),
        lax.all_gather(right_cols[None], "row", axis=0, tiled=True),
    )
    right_vals, right_cols, values = lax.optimization_barrier((right_vals, right_cols, values))
    right_vals, right_cols = right_rows_vals, right_rows_cols
    left_vals, left_cols = pack_slots(
        values, col_ids, col_ids // group_rows % depths, is_live, depths, cap_left
    )
    left_vals, left_cols = (
        lax.all_to_all(left_vals, "depth", split_axis=0, concat_axis=0, tiled=True),
        lax.all_to_all(left_cols, "depth", split_axis=0, concat_axis=0, tiled=True),
    )
    left_vals, left_cols = (
        lax.all_gather(left_vals[None], "col", axis=0, tiled=True),
        lax.all_gather(left_cols[None], "col", axis=0, tiled=True),
    )
    left_shape = left_cols.shape
    source_col = lax.broadcasted_iota(jnp.int32, left_shape, 0)
    source_depth = lax.broadcasted_iota(jnp.int32, left_shape, 1)
    source_row = lax.broadcasted_iota(jnp.int32, left_shape, 2)
    left_rows = (
        (row_index * depths + source_depth) * group_rows + source_col * rows_dev + source_row
    ).reshape(-1)
    left_flat = left_vals.reshape(-1, block_size, block_size)
    left_ids = left_cols.reshape(-1)
    right_flat = right_vals.reshape(-1, cap_right, block_size, block_size)
    right_ids = right_cols.reshape(-1, cap_right)
    pattern_rows = out_pattern[0, 0, :, 0]
    pattern_cols = out_pattern[0, 0, :, 1]
    local_row = pattern_rows - row_index * (depths * group_rows)
    left_pos = (local_row % group_rows) * depths + local_row // group_rows
    left_sel = left_pos[:, None] * cap_left + jnp.arange(cap_left, dtype=jnp.int32)[None, :]
    left_flat = left_vals.reshape(-1, block_size, block_size)
    left_ids = left_cols.reshape(-1)
    left_pick = jnp.take(left_flat, left_sel.reshape(-1), axis=0)
    inner = jnp.take(left_ids, left_sel, axis=0)
    safe_inner = jnp.maximum(inner, 0)
    right_row = safe_inner // (depths * group_rows) * columns + safe_inner % group_rows
    right_ids = right_cols.reshape(-1, cap_right)
    right_flat = right_vals.reshape(-1, block_size, block_size)
    right_here = jnp.take(right_ids, right_row, axis=0)
    matched = (right_here == pattern_cols[:, None, None]) & (inner >= 0)[:, :, None]
    slot = jnp.sum(
        jnp.where(matched, jnp.arange(cap_right, dtype=jnp.int32)[None, None, :], 0), axis=2
    )
    found = jnp.any(matched, axis=2)
    right_pick = jnp.take(right_flat, (right_row * cap_right + slot).reshape(-1), axis=0)
    right_pick = jnp.where(
        found.reshape(-1)[:, None, None], right_pick, jnp.zeros_like(right_pick)
    )
    pattern_len = pattern_rows.shape[0]
    left_pick = left_pick.reshape(pattern_len, cap_left, block_size, block_size)
    right_pick = right_pick.reshape(pattern_len, cap_left, block_size, block_size)
    partial_sum = jnp.einsum(
        "pqab,pqbc->pac", left_pick, right_pick, preferred_element_type=jnp.float32
    )
    share = lax.psum_scatter(partial_sum[None, None], "depth", scatter_dimension=2, tiled=True)
    return jnp.log1p(share).astype(jnp.bfloat16)


def solution(mesh):
    in_specs = (
        P(("row", "depth"), "col", None, None, None),
        P(("row", "depth"), "col", None),
        P(("row", "depth"), "col"),
        P("row", "col", None, None),
    )
    out_specs = P("row", "col", "depth", None, None)
    return jax.shard_map(body, mesh=mesh, in_specs=in_specs, out_specs=out_specs, check_vma=False)
```

```python
import math

import jax
import jax.numpy as jnp
from jax import lax
from jax.sharding import PartitionSpec as P


def pack_slots(values, col_ids, targets, is_live, part_count, capacity):
    row_count = col_ids.shape[0]
    block_size = values.shape[-1]
    chosen = (
        targets[:, :, None] == jnp.arange(part_count, dtype=jnp.int32)[None, None, :]
    ) & is_live[:, :, None]
    running = jnp.cumsum(chosen.astype(jnp.int32), axis=1) - 1
    order_in = jnp.sum(jnp.where(chosen, running, 0), axis=2)
    row_ids = jnp.arange(row_count, dtype=jnp.int32)[:, None]
    total = part_count * row_count * capacity
    position = (targets * row_count + row_ids) * capacity + order_in
    position = jnp.where(is_live, position, total).reshape(-1)
    packed = jnp.zeros((total, block_size, block_size), values.dtype)
    packed = packed.at[position].set(values.reshape(-1, block_size, block_size), mode="drop")
    packed_cols = (
        jnp.full((total,), -1, jnp.int32).at[position].set(col_ids.reshape(-1), mode="drop")
    )
    return (
        packed.reshape(part_count, row_count, capacity, block_size, block_size),
        packed_cols.reshape(part_count, row_count, capacity),
    )


def gather_by_exchange(x, axis, size):
    copies = jnp.broadcast_to(x[None], (size,) + x.shape)
    return lax.all_to_all(copies, axis, split_axis=0, concat_axis=0, tiled=True)


def body(block_values, block_cols, live_count, out_pattern):
    depths = lax.axis_size("depth")
    columns = lax.axis_size("col")
    row_groups = lax.axis_size("row")
    row_index = lax.axis_index("row")
    rows_dev = block_values.shape[1]
    slot_count = block_values.shape[2]
    block_size = block_values.shape[3]
    group_rows = columns * rows_dev
    group_count = row_groups * depths
    total_rows = group_count * group_rows
    col_block = total_rows // columns
    pair_size = group_count // columns
    cap_left = slot_count // depths
    cap_right = pair_size * (slot_count // group_count) + min(pair_size, slot_count % group_count)
    values = block_values.reshape(rows_dev, slot_count, block_size, block_size)
    col_ids = block_cols.reshape(rows_dev, slot_count)
    counts = live_count.reshape(rows_dev)
    is_live = jnp.arange(slot_count, dtype=jnp.int32)[None, :] < counts[:, None]
    left_vals, left_cols = pack_slots(
        values, col_ids, col_ids // group_rows % depths, is_live, depths, cap_left
    )
    left_vals, left_cols = (
        lax.all_to_all(left_vals, "depth", split_axis=0, concat_axis=0, tiled=True),
        lax.all_to_all(left_cols, "depth", split_axis=0, concat_axis=0, tiled=True),
    )
    left_vals, left_cols = (
        lax.all_gather(left_vals[None], "col", axis=0, tiled=True),
        gather_by_exchange(left_cols, "col", columns),
    )
    left_shape = left_cols.shape
    source_col = lax.broadcasted_iota(jnp.int32, left_shape, 0)
    source_depth = lax.broadcasted_iota(jnp.int32, left_shape, 1)
    source_row = lax.broadcasted_iota(jnp.int32, left_shape, 2)
    left_rows = (
        (row_index * depths + source_depth) * group_rows + source_col * rows_dev + source_row
    ).reshape(-1)
    left_flat = left_vals.reshape(-1, block_size, block_size)
    left_ids = left_cols.reshape(-1)
    right_vals, right_cols = pack_slots(
        values, col_ids, col_ids // col_block, is_live, columns, cap_right
    )
    right_vals, right_cols = (
        lax.all_to_all(right_vals, "col", split_axis=0, concat_axis=0, tiled=True),
        lax.all_to_all(right_cols, "col", split_axis=0, concat_axis=0, tiled=True),
    )
    right_vals, right_cols = (
        lax.all_gather(right_vals[None], "row", axis=0, tiled=True),
        gather_by_exchange(right_cols, "row", row_groups),
    )
    right_flat = right_vals.reshape(-1, cap_right, block_size, block_size)
    right_ids = right_cols.reshape(-1, cap_right)
    pattern_rows = out_pattern[0, 0, :, 0]
    pattern_cols = out_pattern[0, 0, :, 1]
    local_row = pattern_rows - row_index * (depths * group_rows)
    left_pos = (local_row % group_rows) * depths + local_row // group_rows
    left_sel = left_pos[:, None] * cap_left + jnp.arange(cap_left, dtype=jnp.int32)[None, :]
    left_flat = left_vals.reshape(-1, block_size, block_size)
    left_ids = left_cols.reshape(-1)
    left_pick = jnp.take(left_flat, left_sel.reshape(-1), axis=0)
    inner = jnp.take(left_ids, left_sel, axis=0)
    safe_inner = jnp.maximum(inner, 0)
    right_row = safe_inner // (depths * group_rows) * columns + safe_inner % group_rows
    right_ids = right_cols.reshape(-1, cap_right)
    right_flat = right_vals.reshape(-1, block_size, block_size)
    right_here = jnp.take(right_ids, right_row, axis=0)
    matched = (right_here == pattern_cols[:, None, None]) & (inner >= 0)[:, :, None]
    slot = jnp.sum(
        jnp.where(matched, jnp.arange(cap_right, dtype=jnp.int32)[None, None, :], 0), axis=2
    )
    found = jnp.any(matched, axis=2)
    right_pick = jnp.take(right_flat, (right_row * cap_right + slot).reshape(-1), axis=0)
    right_pick = jnp.where(
        found.reshape(-1)[:, None, None], right_pick, jnp.zeros_like(right_pick)
    )
    pattern_len = pattern_rows.shape[0]
    left_pick = left_pick.reshape(pattern_len, cap_left, block_size, block_size)
    right_pick = right_pick.reshape(pattern_len, cap_left, block_size, block_size)
    partial_sum = jnp.einsum(
        "pqab,pqbc->pac", left_pick, right_pick, preferred_element_type=jnp.float32
    )
    share = lax.psum_scatter(partial_sum[None, None], "depth", scatter_dimension=2, tiled=True)
    return jnp.log1p(share).astype(jnp.bfloat16)


def solution(mesh):
    in_specs = (
        P(("row", "depth"), "col", None, None, None),
        P(("row", "depth"), "col", None),
        P(("row", "depth"), "col"),
        P("row", "col", None, None),
    )
    out_specs = P("row", "col", "depth", None, None)
    return jax.shard_map(body, mesh=mesh, in_specs=in_specs, out_specs=out_specs, check_vma=False)
```

```python
import math

import jax
import jax.numpy as jnp
from jax import lax
from jax.sharding import PartitionSpec as P


def pack_slots(values, col_ids, targets, is_live, part_count, capacity):
    row_count = col_ids.shape[0]
    block_size = values.shape[-1]
    chosen = (
        targets[:, :, None] == jnp.arange(part_count, dtype=jnp.int32)[None, None, :]
    ) & is_live[:, :, None]
    running = jnp.cumsum(chosen.astype(jnp.int32), axis=1) - 1
    order_in = jnp.sum(jnp.where(chosen, running, 0), axis=2)
    row_ids = jnp.arange(row_count, dtype=jnp.int32)[:, None]
    total = part_count * row_count * capacity
    position = (targets * row_count + row_ids) * capacity + order_in
    position = jnp.where(is_live, position, total).reshape(-1)
    packed = jnp.zeros((total, block_size, block_size), values.dtype)
    packed = packed.at[position].set(values.reshape(-1, block_size, block_size), mode="drop")
    packed_cols = (
        jnp.full((total,), -1, jnp.int32).at[position].set(col_ids.reshape(-1), mode="drop")
    )
    return (
        packed.reshape(part_count, row_count, capacity, block_size, block_size),
        packed_cols.reshape(part_count, row_count, capacity),
    )


def gather_by_exchange(x, axis, size):
    copies = jnp.broadcast_to(x[None], (size,) + x.shape)
    return lax.all_to_all(copies, axis, split_axis=0, concat_axis=0, tiled=True)


def body(block_values, block_cols, live_count, out_pattern):
    depths = lax.axis_size("depth")
    columns = lax.axis_size("col")
    row_groups = lax.axis_size("row")
    row_index = lax.axis_index("row")
    rows_dev = block_values.shape[1]
    slot_count = block_values.shape[2]
    block_size = block_values.shape[3]
    group_rows = columns * rows_dev
    group_count = row_groups * depths
    total_rows = group_count * group_rows
    col_block = total_rows // columns
    pair_size = group_count // columns
    cap_left = slot_count // depths
    cap_right = pair_size * (slot_count // group_count) + min(pair_size, slot_count % group_count)
    values = block_values.reshape(rows_dev, slot_count, block_size, block_size)
    col_ids = block_cols.reshape(rows_dev, slot_count)
    counts = live_count.reshape(rows_dev)
    is_live = jnp.arange(slot_count, dtype=jnp.int32)[None, :] < counts[:, None]
    left_vals, left_cols = pack_slots(
        values, col_ids, col_ids // group_rows % depths, is_live, depths, cap_left
    )
    left_vals, left_cols = (
        lax.all_to_all(left_vals, "depth", split_axis=0, concat_axis=0, tiled=True),
        lax.all_to_all(left_cols, "depth", split_axis=0, concat_axis=0, tiled=True),
    )
    left_vals, left_cols = (
        lax.all_gather(left_vals[None], "col", axis=0, tiled=True),
        gather_by_exchange(left_cols, "col", columns),
    )
    left_shape = left_cols.shape
    source_col = lax.broadcasted_iota(jnp.int32, left_shape, 0)
    source_depth = lax.broadcasted_iota(jnp.int32, left_shape, 1)
    source_row = lax.broadcasted_iota(jnp.int32, left_shape, 2)
    left_rows = (
        (row_index * depths + source_depth) * group_rows + source_col * rows_dev + source_row
    ).reshape(-1)
    left_flat = left_vals.reshape(-1, block_size, block_size)
    left_ids = left_cols.reshape(-1)
    right_vals, right_cols = pack_slots(
        values, col_ids, col_ids // col_block, is_live, columns, cap_right
    )
    right_vals, right_cols = (
        lax.all_to_all(right_vals, "col", split_axis=0, concat_axis=0, tiled=True),
        lax.all_to_all(right_cols, "col", split_axis=0, concat_axis=0, tiled=True),
    )
    right_vals, right_cols = (
        lax.all_gather(right_vals[None], "row", axis=0, tiled=True),
        gather_by_exchange(right_cols, "row", row_groups),
    )
    right_flat = right_vals.reshape(-1, cap_right, block_size, block_size)
    right_ids = right_cols.reshape(-1, cap_right)
    pattern_rows = out_pattern[0, 0, :, 0]
    pattern_cols = out_pattern[0, 0, :, 1]
    local_row = pattern_rows - row_index * (depths * group_rows)
    left_pos = (local_row % group_rows) * depths + local_row // group_rows
    left_sel = left_pos[:, None] * cap_left + jnp.arange(cap_left, dtype=jnp.int32)[None, :]
    left_flat = left_vals.reshape(-1, block_size, block_size)
    left_ids = left_cols.reshape(-1)
    left_pick = jnp.take(left_flat, left_sel.reshape(-1), axis=0)
    inner = jnp.take(left_ids, left_sel, axis=0)
    safe_inner = jnp.maximum(inner, 0)
    right_row = safe_inner // (depths * group_rows) * columns + safe_inner % group_rows
    right_ids = right_cols.reshape(-1, cap_right)
    right_flat = right_vals.reshape(-1, block_size, block_size)
    right_here = jnp.take(right_ids, right_row, axis=0)
    matched = (right_here == pattern_cols[:, None, None]) & (inner >= 0)[:, :, None]
    slot = jnp.sum(
        jnp.where(matched, jnp.arange(cap_right, dtype=jnp.int32)[None, None, :], 0), axis=2
    )
    found = jnp.any(matched, axis=2)
    right_pick = jnp.take(right_flat, (right_row * cap_right + slot).reshape(-1), axis=0)
    right_pick = jnp.where(
        found.reshape(-1)[:, None, None], right_pick, jnp.zeros_like(right_pick)
    )
    pattern_len = pattern_rows.shape[0]
    left_pick = left_pick.reshape(pattern_len, cap_left, block_size, block_size)
    right_pick = right_pick.reshape(pattern_len, cap_left, block_size, block_size)
    partial_sum = jnp.einsum(
        "pqab,pqbc->pac", left_pick, right_pick, preferred_element_type=jnp.float32
    )
    pieces = lax.all_to_all(
        partial_sum.reshape(depths, pattern_len // depths, block_size, block_size),
        "depth",
        split_axis=0,
        concat_axis=0,
        tiled=True,
    )
    share = jnp.sum(pieces, axis=0)[None, None]
    return jnp.log1p(share).astype(jnp.bfloat16)


def solution(mesh):
    in_specs = (
        P(("row", "depth"), "col", None, None, None),
        P(("row", "depth"), "col", None),
        P(("row", "depth"), "col"),
        P("row", "col", None, None),
    )
    out_specs = P("row", "col", "depth", None, None)
    return jax.shard_map(body, mesh=mesh, in_specs=in_specs, out_specs=out_specs, check_vma=False)
```

```python
import math

import jax
import jax.numpy as jnp
from jax import lax
from jax.sharding import PartitionSpec as P


def pack_slots(values, col_ids, targets, is_live, part_count, capacity):
    row_count = col_ids.shape[0]
    block_size = values.shape[-1]
    chosen = (
        targets[:, :, None] == jnp.arange(part_count, dtype=jnp.int32)[None, None, :]
    ) & is_live[:, :, None]
    running = jnp.cumsum(chosen.astype(jnp.int32), axis=1) - 1
    order_in = jnp.sum(jnp.where(chosen, running, 0), axis=2)
    row_ids = jnp.arange(row_count, dtype=jnp.int32)[:, None]
    total = part_count * row_count * capacity
    position = (targets * row_count + row_ids) * capacity + order_in
    position = jnp.where(is_live, position, total).reshape(-1)
    packed = jnp.zeros((total, block_size, block_size), values.dtype)
    packed = packed.at[position].set(values.reshape(-1, block_size, block_size), mode="drop")
    packed_cols = (
        jnp.full((total,), -1, jnp.int32).at[position].set(col_ids.reshape(-1), mode="drop")
    )
    return (
        packed.reshape(part_count, row_count, capacity, block_size, block_size),
        packed_cols.reshape(part_count, row_count, capacity),
    )


def gather_by_exchange(x, axis, size):
    copies = jnp.broadcast_to(x[None], (size,) + x.shape)
    return lax.all_to_all(copies, axis, split_axis=0, concat_axis=0, tiled=True)


def body(block_values, block_cols, live_count, out_pattern):
    depths = lax.axis_size("depth")
    columns = lax.axis_size("col")
    row_groups = lax.axis_size("row")
    row_index = lax.axis_index("row")
    rows_dev = block_values.shape[1]
    slot_count = block_values.shape[2]
    block_size = block_values.shape[3]
    group_rows = columns * rows_dev
    group_count = row_groups * depths
    total_rows = group_count * group_rows
    col_block = total_rows // columns
    pair_size = group_count // columns
    cap_left = slot_count // depths
    cap_right = pair_size * (slot_count // group_count) + min(pair_size, slot_count % group_count)
    values = block_values.reshape(rows_dev, slot_count, block_size, block_size)
    col_ids = block_cols.reshape(rows_dev, slot_count)
    counts = live_count.reshape(rows_dev)
    is_live = jnp.arange(slot_count, dtype=jnp.int32)[None, :] < counts[:, None]
    left_vals, left_cols = pack_slots(
        values, col_ids, col_ids // group_rows % depths, is_live, depths, cap_left
    )
    left_vals, left_cols = (
        lax.all_to_all(left_vals, "depth", split_axis=0, concat_axis=0, tiled=True),
        lax.all_to_all(left_cols, "depth", split_axis=0, concat_axis=0, tiled=True),
    )
    right_vals, right_cols = pack_slots(
        values, col_ids, col_ids // col_block, is_live, columns, cap_right
    )
    right_vals, right_cols = (
        lax.all_to_all(right_vals, "col", split_axis=0, concat_axis=0, tiled=True),
        lax.all_to_all(right_cols, "col", split_axis=0, concat_axis=0, tiled=True),
    )
    left_vals, right_vals = lax.optimization_barrier((left_vals, right_vals))
    left_vals, left_cols = (
        lax.all_gather(left_vals[None], "col", axis=0, tiled=True),
        gather_by_exchange(left_cols, "col", columns),
    )
    left_shape = left_cols.shape
    source_col = lax.broadcasted_iota(jnp.int32, left_shape, 0)
    source_depth = lax.broadcasted_iota(jnp.int32, left_shape, 1)
    source_row = lax.broadcasted_iota(jnp.int32, left_shape, 2)
    left_rows = (
        (row_index * depths + source_depth) * group_rows + source_col * rows_dev + source_row
    ).reshape(-1)
    left_flat = left_vals.reshape(-1, block_size, block_size)
    left_ids = left_cols.reshape(-1)
    right_vals, right_cols = (
        lax.all_gather(right_vals[None], "row", axis=0, tiled=True),
        gather_by_exchange(right_cols, "row", row_groups),
    )
    right_flat = right_vals.reshape(-1, cap_right, block_size, block_size)
    right_ids = right_cols.reshape(-1, cap_right)
    pattern_rows = out_pattern[0, 0, :, 0]
    pattern_cols = out_pattern[0, 0, :, 1]
    local_row = pattern_rows - row_index * (depths * group_rows)
    left_pos = (local_row % group_rows) * depths + local_row // group_rows
    left_sel = left_pos[:, None] * cap_left + jnp.arange(cap_left, dtype=jnp.int32)[None, :]
    left_flat = left_vals.reshape(-1, block_size, block_size)
    left_ids = left_cols.reshape(-1)
    left_pick = jnp.take(left_flat, left_sel.reshape(-1), axis=0)
    inner = jnp.take(left_ids, left_sel, axis=0)
    safe_inner = jnp.maximum(inner, 0)
    right_row = safe_inner // (depths * group_rows) * columns + safe_inner % group_rows
    right_ids = right_cols.reshape(-1, cap_right)
    right_flat = right_vals.reshape(-1, block_size, block_size)
    right_here = jnp.take(right_ids, right_row, axis=0)
    matched = (right_here == pattern_cols[:, None, None]) & (inner >= 0)[:, :, None]
    slot = jnp.sum(
        jnp.where(matched, jnp.arange(cap_right, dtype=jnp.int32)[None, None, :], 0), axis=2
    )
    found = jnp.any(matched, axis=2)
    right_pick = jnp.take(right_flat, (right_row * cap_right + slot).reshape(-1), axis=0)
    right_pick = jnp.where(
        found.reshape(-1)[:, None, None], right_pick, jnp.zeros_like(right_pick)
    )
    pattern_len = pattern_rows.shape[0]
    left_pick = left_pick.reshape(pattern_len, cap_left, block_size, block_size)
    right_pick = right_pick.reshape(pattern_len, cap_left, block_size, block_size)
    partial_sum = jnp.einsum(
        "pqab,pqbc->pac", left_pick, right_pick, preferred_element_type=jnp.float32
    )
    share = lax.psum_scatter(partial_sum[None, None], "depth", scatter_dimension=2, tiled=True)
    return jnp.log1p(share).astype(jnp.bfloat16)


def solution(mesh):
    in_specs = (
        P(("row", "depth"), "col", None, None, None),
        P(("row", "depth"), "col", None),
        P(("row", "depth"), "col"),
        P("row", "col", None, None),
    )
    out_specs = P("row", "col", "depth", None, None)
    return jax.shard_map(body, mesh=mesh, in_specs=in_specs, out_specs=out_specs, check_vma=False)
```

```python
import math

import jax
import jax.numpy as jnp
from jax import lax
from jax.sharding import PartitionSpec as P


def pack_slots(values, col_ids, targets, is_live, part_count, capacity):
    row_count = col_ids.shape[0]
    block_size = values.shape[-1]
    chosen = (
        targets[:, :, None] == jnp.arange(part_count, dtype=jnp.int32)[None, None, :]
    ) & is_live[:, :, None]
    running = jnp.cumsum(chosen.astype(jnp.int32), axis=1) - 1
    order_in = jnp.sum(jnp.where(chosen, running, 0), axis=2)
    row_ids = jnp.arange(row_count, dtype=jnp.int32)[:, None]
    total = part_count * row_count * capacity
    position = (targets * row_count + row_ids) * capacity + order_in
    position = jnp.where(is_live, position, total).reshape(-1)
    packed = jnp.zeros((total, block_size, block_size), values.dtype)
    packed = packed.at[position].set(values.reshape(-1, block_size, block_size), mode="drop")
    packed_cols = (
        jnp.full((total,), -1, jnp.int32).at[position].set(col_ids.reshape(-1), mode="drop")
    )
    return (
        packed.reshape(part_count, row_count, capacity, block_size, block_size),
        packed_cols.reshape(part_count, row_count, capacity),
    )


def gather_by_exchange(x, axis, size):
    copies = jnp.broadcast_to(x[None], (size,) + x.shape)
    return lax.all_to_all(copies, axis, split_axis=0, concat_axis=0, tiled=True)


def body(block_values, block_cols, live_count, out_pattern):
    depths = lax.axis_size("depth")
    columns = lax.axis_size("col")
    row_groups = lax.axis_size("row")
    row_index = lax.axis_index("row")
    rows_dev = block_values.shape[1]
    slot_count = block_values.shape[2]
    block_size = block_values.shape[3]
    group_rows = columns * rows_dev
    group_count = row_groups * depths
    total_rows = group_count * group_rows
    col_block = total_rows // columns
    pair_size = group_count // columns
    cap_left = slot_count // depths
    cap_right = pair_size * (slot_count // group_count) + min(pair_size, slot_count % group_count)
    values = block_values.reshape(rows_dev, slot_count, block_size, block_size)
    col_ids = block_cols.reshape(rows_dev, slot_count)
    counts = live_count.reshape(rows_dev)
    is_live = jnp.arange(slot_count, dtype=jnp.int32)[None, :] < counts[:, None]
    left_vals, left_cols = pack_slots(
        values, col_ids, col_ids // group_rows % depths, is_live, depths, cap_left
    )
    left_vals, left_cols = (
        lax.all_to_all(left_vals, "depth", split_axis=0, concat_axis=0, tiled=True),
        lax.all_to_all(left_cols, "depth", split_axis=0, concat_axis=0, tiled=True),
    )
    right_vals, right_cols = pack_slots(
        values, col_ids, col_ids // col_block, is_live, columns, cap_right
    )
    right_vals, right_cols = (
        lax.all_to_all(right_vals, "col", split_axis=0, concat_axis=0, tiled=True),
        lax.all_to_all(right_cols, "col", split_axis=0, concat_axis=0, tiled=True),
    )
    left_vals, left_cols = (
        lax.all_gather(left_vals[None], "col", axis=0, tiled=True),
        gather_by_exchange(left_cols, "col", columns),
    )
    left_shape = left_cols.shape
    source_col = lax.broadcasted_iota(jnp.int32, left_shape, 0)
    source_depth = lax.broadcasted_iota(jnp.int32, left_shape, 1)
    source_row = lax.broadcasted_iota(jnp.int32, left_shape, 2)
    left_rows = (
        (row_index * depths + source_depth) * group_rows + source_col * rows_dev + source_row
    ).reshape(-1)
    left_flat = left_vals.reshape(-1, block_size, block_size)
    left_ids = left_cols.reshape(-1)
    right_vals, left_vals = lax.optimization_barrier((right_vals, left_vals))
    right_vals, right_cols = (
        lax.all_gather(right_vals[None], "row", axis=0, tiled=True),
        gather_by_exchange(right_cols, "row", row_groups),
    )
    right_flat = right_vals.reshape(-1, cap_right, block_size, block_size)
    right_ids = right_cols.reshape(-1, cap_right)
    pattern_rows = out_pattern[0, 0, :, 0]
    pattern_cols = out_pattern[0, 0, :, 1]
    local_row = pattern_rows - row_index * (depths * group_rows)
    left_pos = (local_row % group_rows) * depths + local_row // group_rows
    left_sel = left_pos[:, None] * cap_left + jnp.arange(cap_left, dtype=jnp.int32)[None, :]
    left_flat = left_vals.reshape(-1, block_size, block_size)
    left_ids = left_cols.reshape(-1)
    left_pick = jnp.take(left_flat, left_sel.reshape(-1), axis=0)
    inner = jnp.take(left_ids, left_sel, axis=0)
    safe_inner = jnp.maximum(inner, 0)
    right_row = safe_inner // (depths * group_rows) * columns + safe_inner % group_rows
    right_ids = right_cols.reshape(-1, cap_right)
    right_flat = right_vals.reshape(-1, block_size, block_size)
    right_here = jnp.take(right_ids, right_row, axis=0)
    matched = (right_here == pattern_cols[:, None, None]) & (inner >= 0)[:, :, None]
    slot = jnp.sum(
        jnp.where(matched, jnp.arange(cap_right, dtype=jnp.int32)[None, None, :], 0), axis=2
    )
    found = jnp.any(matched, axis=2)
    right_pick = jnp.take(right_flat, (right_row * cap_right + slot).reshape(-1), axis=0)
    right_pick = jnp.where(
        found.reshape(-1)[:, None, None], right_pick, jnp.zeros_like(right_pick)
    )
    pattern_len = pattern_rows.shape[0]
    left_pick = left_pick.reshape(pattern_len, cap_left, block_size, block_size)
    right_pick = right_pick.reshape(pattern_len, cap_left, block_size, block_size)
    partial_sum = jnp.einsum(
        "pqab,pqbc->pac", left_pick, right_pick, preferred_element_type=jnp.float32
    )
    share = lax.psum_scatter(partial_sum[None, None], "depth", scatter_dimension=2, tiled=True)
    return jnp.log1p(share).astype(jnp.bfloat16)


def solution(mesh):
    in_specs = (
        P(("row", "depth"), "col", None, None, None),
        P(("row", "depth"), "col", None),
        P(("row", "depth"), "col"),
        P("row", "col", None, None),
    )
    out_specs = P("row", "col", "depth", None, None)
    return jax.shard_map(body, mesh=mesh, in_specs=in_specs, out_specs=out_specs, check_vma=False)
```

```python
import jax
import jax.numpy as jnp
from jax import lax
from jax.sharding import PartitionSpec as P

ID_ROWS = 16
ID_BASE = 32


def pack_slots(values, col_ids, targets, is_live, part_count, capacity):
    slot_count = col_ids.shape[0]
    block_size = values.shape[-1]
    chosen = (targets[:, None] == jnp.arange(part_count, dtype=jnp.int32)[None, :]) & is_live[:, None]
    running = jnp.cumsum(chosen.astype(jnp.int32), axis=0) - 1
    order_in = jnp.sum(jnp.where(chosen, running, 0), axis=1)
    total = part_count * capacity
    position = jnp.where(is_live, targets * capacity + order_in, total)
    packed = jnp.zeros((total, block_size, block_size), values.dtype)
    packed = packed.at[position].set(values, mode="drop")
    packed_cols = jnp.full((total,), -1, jnp.int32).at[position].set(col_ids, mode="drop")
    high = packed_cols // ID_BASE
    low = packed_cols - high * ID_BASE
    codes = jnp.stack([high, low]).reshape(2, part_count, capacity).transpose(1, 0, 2)
    id_rows = jnp.zeros((part_count, ID_ROWS, block_size), values.dtype)
    id_rows = id_rows.at[:, :2, :capacity].set(codes.astype(values.dtype))
    return jnp.concatenate(
        [packed.reshape(part_count, capacity * block_size, block_size), id_rows], axis=1
    )


def unpack_ids(payload, capacity, block_size):
    codes = payload[..., capacity * block_size : capacity * block_size + 2, :capacity]
    codes = codes.astype(jnp.int32)
    return codes[..., 0, :] * ID_BASE + codes[..., 1, :]


def body(block_values, block_cols, live_count, out_pattern):
    depths = lax.axis_size("depth")
    columns = lax.axis_size("col")
    row_groups = lax.axis_size("row")
    row_index = lax.axis_index("row")
    slot_count = block_values.shape[2]
    block_size = block_values.shape[3]
    group_rows = columns
    plane_rows = depths * group_rows
    col_block = row_groups * plane_rows // columns
    cap_left = slot_count // depths
    cap_right = 2
    values = block_values.reshape(slot_count, block_size, block_size)
    col_ids = block_cols.reshape(slot_count)
    is_live = jnp.arange(slot_count, dtype=jnp.int32) < live_count.reshape(())

    left = pack_slots(values, col_ids, col_ids // group_rows % depths, is_live, depths, cap_left)
    left = lax.all_to_all(left, "depth", split_axis=0, concat_axis=0, tiled=True)
    right = pack_slots(values, col_ids, col_ids // col_block, is_live, columns, cap_right)
    right = lax.all_to_all(right, "col", split_axis=0, concat_axis=0, tiled=True)
    left = lax.all_gather(left[None], "col", axis=0, tiled=True)
    right, left = lax.optimization_barrier((right, left))
    right = lax.all_gather(right[None], "row", axis=0, tiled=True)

    payload_rows = left.shape[-2]
    left_rows = left.reshape(-1, payload_rows, block_size)
    right_rows = right.reshape(-1, payload_rows, block_size)

    pattern_rows = out_pattern[0, 0, :, 0]
    pattern_cols = out_pattern[0, 0, :, 1]
    pattern_len = pattern_rows.shape[0]
    local_row = pattern_rows - row_index * plane_rows
    left_pos = (local_row % group_rows) * depths + local_row // group_rows
    left_picked = jnp.take(left_rows, left_pos, axis=0)
    inner = unpack_ids(left_picked, cap_left, block_size)
    left_pick = left_picked[:, : cap_left * block_size, :].reshape(
        pattern_len, cap_left, block_size, block_size
    )

    right_ids = unpack_ids(right_rows, cap_right, block_size)
    safe_inner = jnp.maximum(inner, 0)
    right_row = safe_inner // plane_rows * columns + safe_inner % group_rows
    right_here = jnp.take(right_ids, right_row, axis=0)
    matched = (right_here == pattern_cols[:, None, None]) & (inner >= 0)[:, :, None]
    found = jnp.any(matched, axis=2)
    second = matched[:, :, 1]
    right_picked = jnp.take(right_rows, right_row.reshape(-1), axis=0)
    first_block = right_picked[:, :block_size, :]
    second_block = right_picked[:, block_size : 2 * block_size, :]
    right_pick = jnp.where(second.reshape(-1)[:, None, None], second_block, first_block)
    right_pick = jnp.where(
        found.reshape(-1)[:, None, None], right_pick, jnp.zeros_like(right_pick)
    )
    right_pick = right_pick.reshape(pattern_len, cap_left, block_size, block_size)
    partial_sum = jnp.einsum(
        "pqab,pqbc->pac", left_pick, right_pick, preferred_element_type=jnp.float32
    )
    share = lax.psum_scatter(partial_sum[None, None], "depth", scatter_dimension=2, tiled=True)
    return jnp.log1p(share).astype(jnp.bfloat16)


def solution(mesh):
    in_specs = (
        P(("row", "depth"), "col", None, None, None),
        P(("row", "depth"), "col", None),
        P(("row", "depth"), "col"),
        P("row", "col", None, None),
    )
    out_specs = P("row", "col", "depth", None, None)
    return jax.shard_map(body, mesh=mesh, in_specs=in_specs, out_specs=out_specs, check_vma=False)
```

```python
import math

import jax
import jax.numpy as jnp
from jax import lax
from jax.experimental import pallas as pl
from jax.experimental.pallas import tpu as pltpu
from jax.sharding import PartitionSpec as P


def pack_slots(values, col_ids, targets, is_live, part_count, capacity):
    row_count = col_ids.shape[0]
    block_size = values.shape[-1]
    chosen = (
        targets[:, :, None] == jnp.arange(part_count, dtype=jnp.int32)[None, None, :]
    ) & is_live[:, :, None]
    running = jnp.cumsum(chosen.astype(jnp.int32), axis=1) - 1
    order_in = jnp.sum(jnp.where(chosen, running, 0), axis=2)
    row_ids = jnp.arange(row_count, dtype=jnp.int32)[:, None]
    total = part_count * row_count * capacity
    position = (targets * row_count + row_ids) * capacity + order_in
    position = jnp.where(is_live, position, total).reshape(-1)
    packed = jnp.zeros((total, block_size, block_size), values.dtype)
    packed = packed.at[position].set(values.reshape(-1, block_size, block_size), mode="drop")
    packed_cols = (
        jnp.full((total,), -1, jnp.int32).at[position].set(col_ids.reshape(-1), mode="drop")
    )
    return (
        packed.reshape(part_count, row_count, capacity, block_size, block_size),
        packed_cols.reshape(part_count, row_count, capacity),
    )


def gather_by_exchange(x, axis, size):
    copies = jnp.broadcast_to(x[None], (size,) + x.shape)
    return lax.all_to_all(copies, axis, split_axis=0, concat_axis=0, tiled=True)


def pair_kernel(right_index, found, left_ref, right_hbm, out_ref, right_buf, sems):
    count = right_buf.shape[0]
    copies = [
        pltpu.make_async_copy(right_hbm.at[right_index[t]], right_buf.at[t], sems.at[t])
        for t in range(count)
    ]
    for copy in copies:
        copy.start()
    for copy in copies:
        copy.wait()
    for p in range(count // 2):
        total = jnp.zeros(out_ref.shape[1:], jnp.float32)
        for t in (2 * p, 2 * p + 1):
            term = jnp.dot(left_ref[t], right_buf[t], preferred_element_type=jnp.float32)
            total = total + jnp.where(found[t] != 0, term, 0.0)
        out_ref[p] = total


def pair_products(right_index, found, left_pick, right_flat):
    count, block_size, _ = left_pick.shape
    return pl.pallas_call(
        pair_kernel,
        out_shape=jax.ShapeDtypeStruct((count // 2, block_size, block_size), jnp.float32),
        in_specs=[
            pl.BlockSpec(memory_space=pltpu.SMEM),
            pl.BlockSpec(memory_space=pltpu.SMEM),
            pl.BlockSpec(memory_space=pltpu.VMEM),
            pl.BlockSpec(memory_space=pl.ANY),
        ],
        out_specs=pl.BlockSpec(memory_space=pltpu.VMEM),
        scratch_shapes=[
            pltpu.VMEM((count, block_size, block_size), right_flat.dtype),
            pltpu.SemaphoreType.DMA((count,)),
        ],
        cost_estimate=pl.CostEstimate(
            flops=2 * count * block_size**3,
            bytes_accessed=count * block_size * block_size * 2 * 2 + count * block_size * block_size * 2,
            transcendentals=0,
        ),
    )(right_index, found, left_pick, right_flat)


def body(block_values, block_cols, live_count, out_pattern):
    depths = lax.axis_size("depth")
    columns = lax.axis_size("col")
    row_groups = lax.axis_size("row")
    row_index = lax.axis_index("row")
    rows_dev = block_values.shape[1]
    slot_count = block_values.shape[2]
    block_size = block_values.shape[3]
    group_rows = columns * rows_dev
    group_count = row_groups * depths
    total_rows = group_count * group_rows
    col_block = total_rows // columns
    pair_size = group_count // columns
    cap_left = slot_count // depths
    cap_right = pair_size * (slot_count // group_count) + min(pair_size, slot_count % group_count)
    values = block_values.reshape(rows_dev, slot_count, block_size, block_size)
    col_ids = block_cols.reshape(rows_dev, slot_count)
    counts = live_count.reshape(rows_dev)
    is_live = jnp.arange(slot_count, dtype=jnp.int32)[None, :] < counts[:, None]
    left_vals, left_cols = pack_slots(
        values, col_ids, col_ids // group_rows % depths, is_live, depths, cap_left
    )
    left_vals, left_cols = (
        lax.all_to_all(left_vals, "depth", split_axis=0, concat_axis=0, tiled=True),
        lax.all_to_all(left_cols, "depth", split_axis=0, concat_axis=0, tiled=True),
    )
    left_vals, left_cols = (
        lax.all_gather(left_vals[None], "col", axis=0, tiled=True),
        gather_by_exchange(left_cols, "col", columns),
    )
    left_shape = left_cols.shape
    source_col = lax.broadcasted_iota(jnp.int32, left_shape, 0)
    source_depth = lax.broadcasted_iota(jnp.int32, left_shape, 1)
    source_row = lax.broadcasted_iota(jnp.int32, left_shape, 2)
    left_rows = (
        (row_index * depths + source_depth) * group_rows + source_col * rows_dev + source_row
    ).reshape(-1)
    left_flat = left_vals.reshape(-1, block_size, block_size)
    left_ids = left_cols.reshape(-1)
    right_vals, right_cols = pack_slots(
        values, col_ids, col_ids // col_block, is_live, columns, cap_right
    )
    right_vals, right_cols = (
        lax.all_to_all(right_vals, "col", split_axis=0, concat_axis=0, tiled=True),
        lax.all_to_all(right_cols, "col", split_axis=0, concat_axis=0, tiled=True),
    )
    right_vals, right_cols = (
        lax.all_gather(right_vals[None], "row", axis=0, tiled=True),
        gather_by_exchange(right_cols, "row", row_groups),
    )
    right_flat = right_vals.reshape(-1, cap_right, block_size, block_size)
    right_ids = right_cols.reshape(-1, cap_right)
    pattern_rows = out_pattern[0, 0, :, 0]
    pattern_cols = out_pattern[0, 0, :, 1]
    local_row = pattern_rows - row_index * (depths * group_rows)
    left_pos = (local_row % group_rows) * depths + local_row // group_rows
    left_sel = left_pos[:, None] * cap_left + jnp.arange(cap_left, dtype=jnp.int32)[None, :]
    left_flat = left_vals.reshape(-1, block_size, block_size)
    left_ids = left_cols.reshape(-1)
    left_pick = jnp.take(left_flat, left_sel.reshape(-1), axis=0)
    inner = jnp.take(left_ids, left_sel, axis=0)
    safe_inner = jnp.maximum(inner, 0)
    right_row = safe_inner // (depths * group_rows) * columns + safe_inner % group_rows
    right_ids = right_cols.reshape(-1, cap_right)
    right_flat = right_vals.reshape(-1, block_size, block_size)
    right_here = jnp.take(right_ids, right_row, axis=0)
    matched = (right_here == pattern_cols[:, None, None]) & (inner >= 0)[:, :, None]
    slot = jnp.sum(
        jnp.where(matched, jnp.arange(cap_right, dtype=jnp.int32)[None, None, :], 0), axis=2
    )
    found = jnp.any(matched, axis=2)
    pattern_len = pattern_rows.shape[0]
    partial_sum = pair_products(
        (right_row * cap_right + slot).reshape(-1),
        found.reshape(-1).astype(jnp.int32),
        left_pick,
        right_flat,
    ).reshape(pattern_len, block_size, block_size)
    share = lax.psum_scatter(partial_sum[None, None], "depth", scatter_dimension=2, tiled=True)
    return jnp.log1p(share).astype(jnp.bfloat16)


def solution(mesh):
    in_specs = (
        P(("row", "depth"), "col", None, None, None),
        P(("row", "depth"), "col", None),
        P(("row", "depth"), "col"),
        P("row", "col", None, None),
    )
    out_specs = P("row", "col", "depth", None, None)
    return jax.shard_map(body, mesh=mesh, in_specs=in_specs, out_specs=out_specs, check_vma=False)
```

```python
import math

import jax
import jax.numpy as jnp
from jax import lax
from jax.experimental import pallas as pl
from jax.experimental.pallas import tpu as pltpu
from jax.sharding import PartitionSpec as P


def pack_slots(values, col_ids, targets, is_live, part_count, capacity):
    row_count = col_ids.shape[0]
    block_size = values.shape[-1]
    chosen = (
        targets[:, :, None] == jnp.arange(part_count, dtype=jnp.int32)[None, None, :]
    ) & is_live[:, :, None]
    running = jnp.cumsum(chosen.astype(jnp.int32), axis=1) - 1
    order_in = jnp.sum(jnp.where(chosen, running, 0), axis=2)
    row_ids = jnp.arange(row_count, dtype=jnp.int32)[:, None]
    total = part_count * row_count * capacity
    position = (targets * row_count + row_ids) * capacity + order_in
    position = jnp.where(is_live, position, total).reshape(-1)
    packed = jnp.zeros((total, block_size, block_size), values.dtype)
    packed = packed.at[position].set(values.reshape(-1, block_size, block_size), mode="drop")
    packed_cols = (
        jnp.full((total,), -1, jnp.int32).at[position].set(col_ids.reshape(-1), mode="drop")
    )
    return (
        packed.reshape(part_count, row_count, capacity, block_size, block_size),
        packed_cols.reshape(part_count, row_count, capacity),
    )


def gather_by_exchange(x, axis, size):
    copies = jnp.broadcast_to(x[None], (size,) + x.shape)
    return lax.all_to_all(copies, axis, split_axis=0, concat_axis=0, tiled=True)


def pair_kernel(right_index, found, left_ref, right_hbm, out_ref, right_buf, sems):
    count = right_buf.shape[0]
    copies = [
        pltpu.make_async_copy(right_hbm.at[right_index[t]], right_buf.at[t], sems.at[t])
        for t in range(count)
    ]
    for copy in copies:
        copy.start()
    for copy in copies:
        copy.wait()
    for p in range(count // 2):
        total = jnp.zeros(out_ref.shape[1:], jnp.float32)
        for t in (2 * p, 2 * p + 1):
            term = jnp.dot(left_ref[t], right_buf[t], preferred_element_type=jnp.float32)
            total = total + jnp.where(found[t] != 0, term, 0.0)
        out_ref[p] = total


def pair_products(right_index, found, left_pick, right_flat):
    count, block_size, _ = left_pick.shape
    return pl.pallas_call(
        pair_kernel,
        out_shape=jax.ShapeDtypeStruct((count // 2, block_size, block_size), jnp.float32),
        in_specs=[
            pl.BlockSpec(memory_space=pltpu.SMEM),
            pl.BlockSpec(memory_space=pltpu.SMEM),
            pl.BlockSpec(memory_space=pltpu.VMEM),
            pl.BlockSpec(memory_space=pl.ANY),
        ],
        out_specs=pl.BlockSpec(memory_space=pltpu.VMEM),
        scratch_shapes=[
            pltpu.VMEM((count, block_size, block_size), right_flat.dtype),
            pltpu.SemaphoreType.DMA((count,)),
        ],
        cost_estimate=pl.CostEstimate(
            flops=2 * count * block_size**3,
            bytes_accessed=count * block_size * block_size * 2 * 2 + count * block_size * block_size * 2,
            transcendentals=0,
        ),
    )(right_index, found, left_pick, right_flat)


def body(block_values, block_cols, live_count, out_pattern):
    depths = lax.axis_size("depth")
    columns = lax.axis_size("col")
    row_groups = lax.axis_size("row")
    row_index = lax.axis_index("row")
    rows_dev = block_values.shape[1]
    slot_count = block_values.shape[2]
    block_size = block_values.shape[3]
    group_rows = columns * rows_dev
    group_count = row_groups * depths
    total_rows = group_count * group_rows
    col_block = total_rows // columns
    pair_size = group_count // columns
    cap_left = slot_count // depths
    cap_right = pair_size * (slot_count // group_count) + min(pair_size, slot_count % group_count)
    values = block_values.reshape(rows_dev, slot_count, block_size, block_size)
    col_ids = block_cols.reshape(rows_dev, slot_count)
    counts = live_count.reshape(rows_dev)
    is_live = jnp.arange(slot_count, dtype=jnp.int32)[None, :] < counts[:, None]
    left_vals, left_cols = pack_slots(
        values, col_ids, col_ids // group_rows % depths, is_live, depths, cap_left
    )
    left_vals, left_cols = (
        lax.all_to_all(left_vals, "depth", split_axis=0, concat_axis=0, tiled=True),
        lax.all_to_all(left_cols, "depth", split_axis=0, concat_axis=0, tiled=True),
    )
    left_vals = lax.all_gather(left_vals[None], "col", axis=0, tiled=True)
    left_shape = left_cols.shape
    source_col = lax.broadcasted_iota(jnp.int32, left_shape, 0)
    source_depth = lax.broadcasted_iota(jnp.int32, left_shape, 1)
    source_row = lax.broadcasted_iota(jnp.int32, left_shape, 2)
    left_rows = (
        (row_index * depths + source_depth) * group_rows + source_col * rows_dev + source_row
    ).reshape(-1)
    left_flat = left_vals.reshape(-1, block_size, block_size)
    left_ids = left_cols.reshape(-1)
    right_vals, right_cols = pack_slots(
        values, col_ids, col_ids // col_block, is_live, columns, cap_right
    )
    right_vals = lax.all_to_all(right_vals, "col", split_axis=0, concat_axis=0, tiled=True)
    left_width = left_cols.size
    id_pack = jnp.concatenate(
        [
            jnp.broadcast_to(left_cols.reshape(1, -1), (columns, left_width)),
            right_cols.reshape(columns, -1),
        ],
        axis=1,
    )
    id_pack = lax.all_to_all(id_pack, "col", split_axis=0, concat_axis=0, tiled=True)
    left_cols = id_pack[:, :left_width].reshape((columns,) + left_cols.shape)
    right_cols = id_pack[:, left_width:].reshape(right_cols.shape)
    right_vals, right_cols = (
        lax.all_gather(right_vals[None], "row", axis=0, tiled=True),
        gather_by_exchange(right_cols, "row", row_groups),
    )
    right_flat = right_vals.reshape(-1, cap_right, block_size, block_size)
    right_ids = right_cols.reshape(-1, cap_right)
    pattern_rows = out_pattern[0, 0, :, 0]
    pattern_cols = out_pattern[0, 0, :, 1]
    local_row = pattern_rows - row_index * (depths * group_rows)
    left_pos = (local_row % group_rows) * depths + local_row // group_rows
    left_sel = left_pos[:, None] * cap_left + jnp.arange(cap_left, dtype=jnp.int32)[None, :]
    left_flat = left_vals.reshape(-1, block_size, block_size)
    left_ids = left_cols.reshape(-1)
    left_pick = jnp.take(left_flat, left_sel.reshape(-1), axis=0)
    inner = jnp.take(left_ids, left_sel, axis=0)
    safe_inner = jnp.maximum(inner, 0)
    right_row = safe_inner // (depths * group_rows) * columns + safe_inner % group_rows
    right_ids = right_cols.reshape(-1, cap_right)
    right_flat = right_vals.reshape(-1, block_size, block_size)
    right_here = jnp.take(right_ids, right_row, axis=0)
    matched = (right_here == pattern_cols[:, None, None]) & (inner >= 0)[:, :, None]
    slot = jnp.sum(
        jnp.where(matched, jnp.arange(cap_right, dtype=jnp.int32)[None, None, :], 0), axis=2
    )
    found = jnp.any(matched, axis=2)
    pattern_len = pattern_rows.shape[0]
    partial_sum = pair_products(
        (right_row * cap_right + slot).reshape(-1),
        found.reshape(-1).astype(jnp.int32),
        left_pick,
        right_flat,
    ).reshape(pattern_len, block_size, block_size)
    share = lax.psum_scatter(partial_sum[None, None], "depth", scatter_dimension=2, tiled=True)
    return jnp.log1p(share).astype(jnp.bfloat16)


def solution(mesh):
    in_specs = (
        P(("row", "depth"), "col", None, None, None),
        P(("row", "depth"), "col", None),
        P(("row", "depth"), "col"),
        P("row", "col", None, None),
    )
    out_specs = P("row", "col", "depth", None, None)
    return jax.shard_map(body, mesh=mesh, in_specs=in_specs, out_specs=out_specs, check_vma=False)
```

```python
import math

import jax
import jax.numpy as jnp
from jax import lax
from jax.experimental import pallas as pl
from jax.experimental.pallas import tpu as pltpu
from jax.sharding import PartitionSpec as P


def pack_slots(values, col_ids, targets, is_live, part_count, capacity):
    row_count = col_ids.shape[0]
    block_size = values.shape[-1]
    chosen = (
        targets[:, :, None] == jnp.arange(part_count, dtype=jnp.int32)[None, None, :]
    ) & is_live[:, :, None]
    running = jnp.cumsum(chosen.astype(jnp.int32), axis=1) - 1
    order_in = jnp.sum(jnp.where(chosen, running, 0), axis=2)
    row_ids = jnp.arange(row_count, dtype=jnp.int32)[:, None]
    total = part_count * row_count * capacity
    position = (targets * row_count + row_ids) * capacity + order_in
    position = jnp.where(is_live, position, total).reshape(-1)
    packed = jnp.zeros((total, block_size, block_size), values.dtype)
    packed = packed.at[position].set(values.reshape(-1, block_size, block_size), mode="drop")
    packed_cols = (
        jnp.full((total,), -1, jnp.int32).at[position].set(col_ids.reshape(-1), mode="drop")
    )
    return (
        packed.reshape(part_count, row_count, capacity, block_size, block_size),
        packed_cols.reshape(part_count, row_count, capacity),
    )


def gather_by_exchange(x, axis, size):
    copies = jnp.broadcast_to(x[None], (size,) + x.shape)
    return lax.all_to_all(copies, axis, split_axis=0, concat_axis=0, tiled=True)


def pair_kernel(right_index, found, left_ref, right_hbm, out_ref, right_buf, sems):
    count = right_buf.shape[0]
    copies = [
        pltpu.make_async_copy(right_hbm.at[right_index[t]], right_buf.at[t], sems.at[t])
        for t in range(count)
    ]
    for copy in copies:
        copy.start()
    for p in range(count // 2):
        total = jnp.zeros(out_ref.shape[1:], jnp.float32)
        for t in (2 * p, 2 * p + 1):
            copies[t].wait()
            term = jnp.dot(left_ref[t], right_buf[t], preferred_element_type=jnp.float32)
            total = total + jnp.where(found[t] != 0, term, 0.0)
        out_ref[p] = total


def pair_products(right_index, found, left_pick, right_flat):
    count, block_size, _ = left_pick.shape
    return pl.pallas_call(
        pair_kernel,
        out_shape=jax.ShapeDtypeStruct((count // 2, block_size, block_size), jnp.float32),
        in_specs=[
            pl.BlockSpec(memory_space=pltpu.SMEM),
            pl.BlockSpec(memory_space=pltpu.SMEM),
            pl.BlockSpec(memory_space=pltpu.VMEM),
            pl.BlockSpec(memory_space=pl.ANY),
        ],
        out_specs=pl.BlockSpec(memory_space=pltpu.VMEM),
        scratch_shapes=[
            pltpu.VMEM((count, block_size, block_size), right_flat.dtype),
            pltpu.SemaphoreType.DMA((count,)),
        ],
        cost_estimate=pl.CostEstimate(
            flops=2 * count * block_size**3,
            bytes_accessed=count * block_size * block_size * 2 * 2 + count * block_size * block_size * 2,
            transcendentals=0,
        ),
    )(right_index, found, left_pick, right_flat)


def body(block_values, block_cols, live_count, out_pattern):
    depths = lax.axis_size("depth")
    columns = lax.axis_size("col")
    row_groups = lax.axis_size("row")
    row_index = lax.axis_index("row")
    rows_dev = block_values.shape[1]
    slot_count = block_values.shape[2]
    block_size = block_values.shape[3]
    group_rows = columns * rows_dev
    group_count = row_groups * depths
    total_rows = group_count * group_rows
    col_block = total_rows // columns
    pair_size = group_count // columns
    cap_left = slot_count // depths
    cap_right = pair_size * (slot_count // group_count) + min(pair_size, slot_count % group_count)
    values = block_values.reshape(rows_dev, slot_count, block_size, block_size)
    col_ids = block_cols.reshape(rows_dev, slot_count)
    counts = live_count.reshape(rows_dev)
    is_live = jnp.arange(slot_count, dtype=jnp.int32)[None, :] < counts[:, None]
    left_vals, left_cols = pack_slots(
        values, col_ids, col_ids // group_rows % depths, is_live, depths, cap_left
    )
    left_vals, left_cols = (
        lax.all_to_all(left_vals, "depth", split_axis=0, concat_axis=0, tiled=True),
        lax.all_to_all(left_cols, "depth", split_axis=0, concat_axis=0, tiled=True),
    )
    left_vals = lax.all_gather(left_vals[None], "col", axis=0, tiled=True)
    left_shape = left_cols.shape
    source_col = lax.broadcasted_iota(jnp.int32, left_shape, 0)
    source_depth = lax.broadcasted_iota(jnp.int32, left_shape, 1)
    source_row = lax.broadcasted_iota(jnp.int32, left_shape, 2)
    left_rows = (
        (row_index * depths + source_depth) * group_rows + source_col * rows_dev + source_row
    ).reshape(-1)
    left_flat = left_vals.reshape(-1, block_size, block_size)
    left_ids = left_cols.reshape(-1)
    right_vals, right_cols = pack_slots(
        values, col_ids, col_ids // col_block, is_live, columns, cap_right
    )
    right_vals = lax.all_to_all(right_vals, "col", split_axis=0, concat_axis=0, tiled=True)
    left_width = left_cols.size
    id_pack = jnp.concatenate(
        [
            jnp.broadcast_to(left_cols.reshape(1, -1), (columns, left_width)),
            right_cols.reshape(columns, -1),
        ],
        axis=1,
    )
    id_pack = lax.all_to_all(id_pack, "col", split_axis=0, concat_axis=0, tiled=True)
    left_cols = id_pack[:, :left_width].reshape((columns,) + left_cols.shape)
    right_cols = id_pack[:, left_width:].reshape(right_cols.shape)
    right_vals, right_cols = (
        lax.all_gather(right_vals[None], "row", axis=0, tiled=True),
        gather_by_exchange(right_cols, "row", row_groups),
    )
    right_flat = right_vals.reshape(-1, cap_right, block_size, block_size)
    right_ids = right_cols.reshape(-1, cap_right)
    pattern_rows = out_pattern[0, 0, :, 0]
    pattern_cols = out_pattern[0, 0, :, 1]
    local_row = pattern_rows - row_index * (depths * group_rows)
    left_pos = (local_row % group_rows) * depths + local_row // group_rows
    left_sel = left_pos[:, None] * cap_left + jnp.arange(cap_left, dtype=jnp.int32)[None, :]
    left_flat = left_vals.reshape(-1, block_size, block_size)
    left_ids = left_cols.reshape(-1)
    left_pick = jnp.take(left_flat, left_sel.reshape(-1), axis=0)
    inner = jnp.take(left_ids, left_sel, axis=0)
    safe_inner = jnp.maximum(inner, 0)
    right_row = safe_inner // (depths * group_rows) * columns + safe_inner % group_rows
    right_ids = right_cols.reshape(-1, cap_right)
    right_flat = right_vals.reshape(-1, block_size, block_size)
    right_here = jnp.take(right_ids, right_row, axis=0)
    matched = (right_here == pattern_cols[:, None, None]) & (inner >= 0)[:, :, None]
    slot = jnp.sum(
        jnp.where(matched, jnp.arange(cap_right, dtype=jnp.int32)[None, None, :], 0), axis=2
    )
    found = jnp.any(matched, axis=2)
    pattern_len = pattern_rows.shape[0]
    partial_sum = pair_products(
        (right_row * cap_right + slot).reshape(-1),
        found.reshape(-1).astype(jnp.int32),
        left_pick,
        right_flat,
    ).reshape(pattern_len, block_size, block_size)
    share = lax.psum_scatter(partial_sum[None, None], "depth", scatter_dimension=2, tiled=True)
    return jnp.log1p(share).astype(jnp.bfloat16)


def solution(mesh):
    in_specs = (
        P(("row", "depth"), "col", None, None, None),
        P(("row", "depth"), "col", None),
        P(("row", "depth"), "col"),
        P("row", "col", None, None),
    )
    out_specs = P("row", "col", "depth", None, None)
    return jax.shard_map(body, mesh=mesh, in_specs=in_specs, out_specs=out_specs, check_vma=False)
```

```python
import math

import jax
import jax.numpy as jnp
from jax import lax
from jax.experimental import pallas as pl
from jax.experimental.pallas import tpu as pltpu
from jax.sharding import PartitionSpec as P


def pack_slots(values, col_ids, targets, is_live, part_count, capacity):
    row_count = col_ids.shape[0]
    block_size = values.shape[-1]
    chosen = (
        targets[:, :, None] == jnp.arange(part_count, dtype=jnp.int32)[None, None, :]
    ) & is_live[:, :, None]
    running = jnp.cumsum(chosen.astype(jnp.int32), axis=1) - 1
    order_in = jnp.sum(jnp.where(chosen, running, 0), axis=2)
    row_ids = jnp.arange(row_count, dtype=jnp.int32)[:, None]
    total = part_count * row_count * capacity
    position = (targets * row_count + row_ids) * capacity + order_in
    position = jnp.where(is_live, position, total).reshape(-1)
    packed = jnp.zeros((total, block_size, block_size), values.dtype)
    packed = packed.at[position].set(values.reshape(-1, block_size, block_size), mode="drop")
    packed_cols = (
        jnp.full((total,), -1, jnp.int32).at[position].set(col_ids.reshape(-1), mode="drop")
    )
    return (
        packed.reshape(part_count, row_count, capacity, block_size, block_size),
        packed_cols.reshape(part_count, row_count, capacity),
    )


def gather_by_exchange(x, axis, size):
    copies = jnp.broadcast_to(x[None], (size,) + x.shape)
    return lax.all_to_all(copies, axis, split_axis=0, concat_axis=0, tiled=True)


def pair_kernel(right_index, left_ref, right_hbm, out_ref, right_buf, sems):
    pairs, width, block_size = right_buf.shape
    per_pair = width // block_size
    copies = [
        pltpu.make_async_copy(
            right_hbm.at[right_index[t]],
            right_buf.at[t // per_pair, pl.ds((t % per_pair) * block_size, block_size)],
            sems.at[t],
        )
        for t in range(pairs * per_pair)
    ]
    for copy in copies:
        copy.start()
    for copy in copies:
        copy.wait()
    for p in range(pairs):
        out_ref[p] = jnp.dot(left_ref[p], right_buf[p], preferred_element_type=jnp.float32)


def pair_products(right_index, left_wide, right_flat):
    pairs, block_size, width = left_wide.shape
    return pl.pallas_call(
        pair_kernel,
        out_shape=jax.ShapeDtypeStruct((pairs, block_size, block_size), jnp.float32),
        in_specs=[
            pl.BlockSpec(memory_space=pltpu.SMEM),
            pl.BlockSpec(memory_space=pltpu.VMEM),
            pl.BlockSpec(memory_space=pl.ANY),
        ],
        out_specs=pl.BlockSpec(memory_space=pltpu.VMEM),
        scratch_shapes=[
            pltpu.VMEM((pairs, width, block_size), right_flat.dtype),
            pltpu.SemaphoreType.DMA((pairs * (width // block_size),)),
        ],
        cost_estimate=pl.CostEstimate(
            flops=2 * pairs * block_size * width * block_size,
            bytes_accessed=pairs * block_size * width * 2 * 2 + pairs * block_size * block_size * 4,
            transcendentals=0,
        ),
    )(right_index, left_wide, right_flat)


def body(block_values, block_cols, live_count, out_pattern):
    depths = lax.axis_size("depth")
    columns = lax.axis_size("col")
    row_groups = lax.axis_size("row")
    row_index = lax.axis_index("row")
    rows_dev = block_values.shape[1]
    slot_count = block_values.shape[2]
    block_size = block_values.shape[3]
    group_rows = columns * rows_dev
    group_count = row_groups * depths
    total_rows = group_count * group_rows
    col_block = total_rows // columns
    pair_size = group_count // columns
    cap_left = slot_count // depths
    cap_right = pair_size * (slot_count // group_count) + min(pair_size, slot_count % group_count)
    values = block_values.reshape(rows_dev, slot_count, block_size, block_size)
    col_ids = block_cols.reshape(rows_dev, slot_count)
    counts = live_count.reshape(rows_dev)
    is_live = jnp.arange(slot_count, dtype=jnp.int32)[None, :] < counts[:, None]
    left_vals, left_cols = pack_slots(
        values, col_ids, col_ids // group_rows % depths, is_live, depths, cap_left
    )
    left_vals, left_cols = (
        lax.all_to_all(left_vals, "depth", split_axis=0, concat_axis=0, tiled=True),
        lax.all_to_all(left_cols, "depth", split_axis=0, concat_axis=0, tiled=True),
    )
    left_vals = lax.all_gather(left_vals[None], "col", axis=0, tiled=True)
    left_shape = left_cols.shape
    source_col = lax.broadcasted_iota(jnp.int32, left_shape, 0)
    source_depth = lax.broadcasted_iota(jnp.int32, left_shape, 1)
    source_row = lax.broadcasted_iota(jnp.int32, left_shape, 2)
    left_rows = (
        (row_index * depths + source_depth) * group_rows + source_col * rows_dev + source_row
    ).reshape(-1)
    left_flat = left_vals.reshape(-1, block_size, block_size)
    left_ids = left_cols.reshape(-1)
    right_vals, right_cols = pack_slots(
        values, col_ids, col_ids // col_block, is_live, columns, cap_right
    )
    right_vals = lax.all_to_all(right_vals, "col", split_axis=0, concat_axis=0, tiled=True)
    left_width = left_cols.size
    id_pack = jnp.concatenate(
        [
            jnp.broadcast_to(left_cols.reshape(1, -1), (columns, left_width)),
            right_cols.reshape(columns, -1),
        ],
        axis=1,
    )
    id_pack = lax.all_to_all(id_pack, "col", split_axis=0, concat_axis=0, tiled=True)
    left_cols = id_pack[:, :left_width].reshape((columns,) + left_cols.shape)
    right_cols = id_pack[:, left_width:].reshape(right_cols.shape)
    right_vals, right_cols = (
        lax.all_gather(right_vals[None], "row", axis=0, tiled=True),
        gather_by_exchange(right_cols, "row", row_groups),
    )
    right_flat = right_vals.reshape(-1, cap_right, block_size, block_size)
    right_ids = right_cols.reshape(-1, cap_right)
    pattern_rows = out_pattern[0, 0, :, 0]
    pattern_cols = out_pattern[0, 0, :, 1]
    local_row = pattern_rows - row_index * (depths * group_rows)
    left_pos = (local_row % group_rows) * depths + local_row // group_rows
    left_sel = left_pos[:, None] * cap_left + jnp.arange(cap_left, dtype=jnp.int32)[None, :]
    left_flat = left_vals.reshape(-1, block_size, block_size)
    left_ids = left_cols.reshape(-1)
    left_pick = jnp.take(left_flat, left_sel.reshape(-1), axis=0)
    inner = jnp.take(left_ids, left_sel, axis=0)
    safe_inner = jnp.maximum(inner, 0)
    right_row = safe_inner // (depths * group_rows) * columns + safe_inner % group_rows
    right_ids = right_cols.reshape(-1, cap_right)
    right_flat = right_vals.reshape(-1, block_size, block_size)
    right_here = jnp.take(right_ids, right_row, axis=0)
    matched = (right_here == pattern_cols[:, None, None]) & (inner >= 0)[:, :, None]
    slot = jnp.sum(
        jnp.where(matched, jnp.arange(cap_right, dtype=jnp.int32)[None, None, :], 0), axis=2
    )
    found = jnp.any(matched, axis=2)
    pattern_len = pattern_rows.shape[0]
    left_wide = jnp.where(
        found.reshape(-1)[:, None, None], left_pick, jnp.zeros_like(left_pick)
    ).reshape(pattern_len, cap_left, block_size, block_size)
    left_wide = left_wide.transpose(0, 2, 1, 3).reshape(pattern_len, block_size, cap_left * block_size)
    partial_sum = pair_products(
        (right_row * cap_right + slot).reshape(-1), left_wide, right_flat
    )
    share = lax.psum_scatter(partial_sum[None, None], "depth", scatter_dimension=2, tiled=True)
    return jnp.log1p(share).astype(jnp.bfloat16)


def solution(mesh):
    in_specs = (
        P(("row", "depth"), "col", None, None, None),
        P(("row", "depth"), "col", None),
        P(("row", "depth"), "col"),
        P("row", "col", None, None),
    )
    out_specs = P("row", "col", "depth", None, None)
    return jax.shard_map(body, mesh=mesh, in_specs=in_specs, out_specs=out_specs, check_vma=False)
```

```python
import math

import jax
import jax.numpy as jnp
from jax import lax
from jax.experimental import pallas as pl
from jax.experimental.pallas import tpu as pltpu
from jax.sharding import PartitionSpec as P


def pack_slots(values, col_ids, targets, is_live, part_count, capacity):
    row_count = col_ids.shape[0]
    block_size = values.shape[-1]
    chosen = (
        targets[:, :, None] == jnp.arange(part_count, dtype=jnp.int32)[None, None, :]
    ) & is_live[:, :, None]
    running = jnp.cumsum(chosen.astype(jnp.int32), axis=1) - 1
    order_in = jnp.sum(jnp.where(chosen, running, 0), axis=2)
    row_ids = jnp.arange(row_count, dtype=jnp.int32)[:, None]
    total = part_count * row_count * capacity
    position = (targets * row_count + row_ids) * capacity + order_in
    position = jnp.where(is_live, position, total).reshape(-1)
    packed = jnp.zeros((total, block_size, block_size), values.dtype)
    packed = packed.at[position].set(values.reshape(-1, block_size, block_size), mode="drop")
    packed_cols = (
        jnp.full((total,), -1, jnp.int32).at[position].set(col_ids.reshape(-1), mode="drop")
    )
    return (
        packed.reshape(part_count, row_count, capacity, block_size, block_size),
        packed_cols.reshape(part_count, row_count, capacity),
    )


def gather_by_exchange(x, axis, size):
    copies = jnp.broadcast_to(x[None], (size,) + x.shape)
    return lax.all_to_all(copies, axis, split_axis=0, concat_axis=0, tiled=True)


def pair_kernel(right_index, found, left_ref, right_hbm, out_ref, right_buf, sems):
    count = right_buf.shape[0]
    copies = [
        pltpu.make_async_copy(right_hbm.at[right_index[t]], right_buf.at[t], sems.at[t])
        for t in range(count)
    ]
    for copy in copies:
        copy.start()
    for copy in copies:
        copy.wait()
    for p in range(count // 2):
        total = jnp.zeros(out_ref.shape[1:], jnp.float32)
        for t in (2 * p, 2 * p + 1):
            term = jnp.dot(left_ref[t], right_buf[t], preferred_element_type=jnp.float32)
            total = total + jnp.where(found[t] != 0, term, 0.0)
        out_ref[p] = total


def pair_products(right_index, found, left_pick, right_flat):
    count, block_size, _ = left_pick.shape
    return pl.pallas_call(
        pair_kernel,
        out_shape=jax.ShapeDtypeStruct((count // 2, block_size, block_size), jnp.float32),
        in_specs=[
            pl.BlockSpec(memory_space=pltpu.SMEM),
            pl.BlockSpec(memory_space=pltpu.SMEM),
            pl.BlockSpec(memory_space=pltpu.VMEM),
            pl.BlockSpec(memory_space=pl.ANY),
        ],
        out_specs=pl.BlockSpec(memory_space=pltpu.VMEM),
        scratch_shapes=[
            pltpu.VMEM((count, block_size, block_size), right_flat.dtype),
            pltpu.SemaphoreType.DMA((count,)),
        ],
        cost_estimate=pl.CostEstimate(
            flops=2 * count * block_size**3,
            bytes_accessed=count * block_size * block_size * 2 * 2 + count * block_size * block_size * 2,
            transcendentals=0,
        ),
    )(right_index, found, left_pick, right_flat)


def body(block_values, block_cols, live_count, out_pattern):
    depths = lax.axis_size("depth")
    columns = lax.axis_size("col")
    row_groups = lax.axis_size("row")
    row_index = lax.axis_index("row")
    rows_dev = block_values.shape[1]
    slot_count = block_values.shape[2]
    block_size = block_values.shape[3]
    group_rows = columns * rows_dev
    group_count = row_groups * depths
    total_rows = group_count * group_rows
    col_block = total_rows // columns
    pair_size = group_count // columns
    cap_left = slot_count // depths
    cap_right = pair_size * (slot_count // group_count) + min(pair_size, slot_count % group_count)
    values = block_values.reshape(rows_dev, slot_count, block_size, block_size)
    col_ids = block_cols.reshape(rows_dev, slot_count)
    counts = live_count.reshape(rows_dev)
    is_live = jnp.arange(slot_count, dtype=jnp.int32)[None, :] < counts[:, None]
    left_vals, left_cols = pack_slots(
        values, col_ids, col_ids // group_rows % depths, is_live, depths, cap_left
    )
    left_vals, left_cols = (
        lax.all_to_all(left_vals, "depth", split_axis=0, concat_axis=0, tiled=True),
        lax.all_to_all(left_cols, "depth", split_axis=0, concat_axis=0, tiled=True),
    )
    left_vals = lax.all_gather(left_vals[None], "col", axis=0, tiled=True)
    left_shape = left_cols.shape
    source_col = lax.broadcasted_iota(jnp.int32, left_shape, 0)
    source_depth = lax.broadcasted_iota(jnp.int32, left_shape, 1)
    source_row = lax.broadcasted_iota(jnp.int32, left_shape, 2)
    left_rows = (
        (row_index * depths + source_depth) * group_rows + source_col * rows_dev + source_row
    ).reshape(-1)
    left_flat = left_vals.reshape(-1, block_size, block_size)
    left_ids = left_cols.reshape(-1)
    right_vals, right_cols = pack_slots(
        values, col_ids, col_ids // col_block, is_live, columns, cap_right
    )
    right_vals = lax.all_to_all(right_vals, "col", split_axis=0, concat_axis=0, tiled=True)
    left_width = left_cols.size
    id_pack = jnp.concatenate(
        [
            jnp.broadcast_to(left_cols.reshape(1, -1), (columns, left_width)),
            right_cols.reshape(columns, -1),
        ],
        axis=1,
    )
    id_pack = lax.all_to_all(id_pack, "col", split_axis=0, concat_axis=0, tiled=True)
    left_cols = id_pack[:, :left_width].reshape((columns,) + left_cols.shape)
    right_cols = id_pack[:, left_width:].reshape(right_cols.shape)
    right_vals, right_cols = (
        lax.all_gather(right_vals[None], "row", axis=0, tiled=True),
        gather_by_exchange(right_cols, "row", row_groups),
    )
    right_flat = right_vals.reshape(-1, cap_right, block_size, block_size)
    right_ids = right_cols.reshape(-1, cap_right)
    pattern_rows = out_pattern[0, 0, :, 0]
    pattern_cols = out_pattern[0, 0, :, 1]
    local_row = pattern_rows - row_index * (depths * group_rows)
    left_pos = (local_row % group_rows) * depths + local_row // group_rows
    left_sel = left_pos[:, None] * cap_left + jnp.arange(cap_left, dtype=jnp.int32)[None, :]
    left_flat = left_vals.reshape(-1, block_size, block_size)
    left_ids = left_cols.reshape(-1)
    left_pick = jnp.take(left_flat, left_sel.reshape(-1), axis=0)
    inner = jnp.take(left_ids, left_sel, axis=0)
    safe_inner = jnp.maximum(inner, 0)
    right_row = safe_inner // (depths * group_rows) * columns + safe_inner % group_rows
    right_ids = right_cols.reshape(-1, cap_right)
    right_flat = right_vals.reshape(-1, block_size, block_size)
    right_here = jnp.take(right_ids, right_row, axis=0)
    matched = (right_here == pattern_cols[:, None, None]) & (inner >= 0)[:, :, None]
    slot = jnp.sum(
        jnp.where(matched, jnp.arange(cap_right, dtype=jnp.int32)[None, None, :], 0), axis=2
    )
    found = jnp.any(matched, axis=2)
    pattern_len = pattern_rows.shape[0]
    partial_sum = pair_products(
        (right_row * cap_right + slot).reshape(-1),
        found.reshape(-1).astype(jnp.int32),
        left_pick,
        right_flat,
    ).reshape(pattern_len, block_size, block_size)
    share = lax.psum_scatter(
        partial_sum.reshape(-1, block_size), "depth", scatter_dimension=0, tiled=True
    ).reshape(1, 1, -1, block_size, block_size)
    return jnp.log1p(share).astype(jnp.bfloat16)


def solution(mesh):
    in_specs = (
        P(("row", "depth"), "col", None, None, None),
        P(("row", "depth"), "col", None),
        P(("row", "depth"), "col"),
        P("row", "col", None, None),
    )
    out_specs = P("row", "col", "depth", None, None)
    return jax.shard_map(body, mesh=mesh, in_specs=in_specs, out_specs=out_specs, check_vma=False)
```

```python
import math

import jax
import jax.numpy as jnp
from jax import lax
from jax.experimental import pallas as pl
from jax.experimental.pallas import tpu as pltpu
from jax.sharding import PartitionSpec as P


def pack_slots(values, col_ids, targets, is_live, part_count, capacity):
    row_count = col_ids.shape[0]
    slot_count = col_ids.shape[1]
    block_size = values.shape[-1]
    chosen = (
        targets[:, :, None] == jnp.arange(part_count, dtype=jnp.int32)[None, None, :]
    ) & is_live[:, :, None]
    running = jnp.cumsum(chosen.astype(jnp.int32), axis=1) - 1
    picks = jnp.arange(capacity, dtype=jnp.int32)
    hit = jnp.transpose(chosen, (0, 2, 1))[:, :, None, :] & (
        jnp.transpose(running, (0, 2, 1))[:, :, None, :] == picks[None, None, :, None]
    )
    slot_ids = jnp.arange(slot_count, dtype=jnp.int32)
    source = jnp.sum(jnp.where(hit, slot_ids, 0), axis=3)
    filled = jnp.any(hit, axis=3)
    row_ids = jnp.arange(row_count, dtype=jnp.int32)[:, None, None]
    flat_source = (row_ids * slot_count + source).reshape(-1)
    blocks = jnp.take(values.reshape(-1, block_size, block_size), flat_source, axis=0)
    blocks = jnp.where(filled.reshape(-1)[:, None, None], blocks, jnp.zeros_like(blocks))
    cols = jnp.where(filled.reshape(-1), jnp.take(col_ids.reshape(-1), flat_source), -1)
    packed = blocks.reshape(row_count, part_count, capacity, block_size, block_size)
    packed_cols = cols.reshape(row_count, part_count, capacity)
    return (
        jnp.transpose(packed, (1, 0, 2, 3, 4)),
        jnp.transpose(packed_cols, (1, 0, 2)),
    )


def gather_by_exchange(x, axis, size):
    copies = jnp.broadcast_to(x[None], (size,) + x.shape)
    return lax.all_to_all(copies, axis, split_axis=0, concat_axis=0, tiled=True)


def pair_kernel(right_index, found, left_ref, right_hbm, out_ref, right_buf, sems):
    count = right_buf.shape[0]
    copies = [
        pltpu.make_async_copy(right_hbm.at[right_index[t]], right_buf.at[t], sems.at[t])
        for t in range(count)
    ]
    for copy in copies:
        copy.start()
    for copy in copies:
        copy.wait()
    for p in range(count // 2):
        total = jnp.zeros(out_ref.shape[1:], jnp.float32)
        for t in (2 * p, 2 * p + 1):
            term = jnp.dot(left_ref[t], right_buf[t], preferred_element_type=jnp.float32)
            total = total + jnp.where(found[t] != 0, term, 0.0)
        out_ref[p] = total


def pair_products(right_index, found, left_pick, right_flat):
    count, block_size, _ = left_pick.shape
    return pl.pallas_call(
        pair_kernel,
        out_shape=jax.ShapeDtypeStruct((count // 2, block_size, block_size), jnp.float32),
        in_specs=[
            pl.BlockSpec(memory_space=pltpu.SMEM),
            pl.BlockSpec(memory_space=pltpu.SMEM),
            pl.BlockSpec(memory_space=pltpu.VMEM),
            pl.BlockSpec(memory_space=pl.ANY),
        ],
        out_specs=pl.BlockSpec(memory_space=pltpu.VMEM),
        scratch_shapes=[
            pltpu.VMEM((count, block_size, block_size), right_flat.dtype),
            pltpu.SemaphoreType.DMA((count,)),
        ],
        cost_estimate=pl.CostEstimate(
            flops=2 * count * block_size**3,
            bytes_accessed=count * block_size * block_size * 2 * 2 + count * block_size * block_size * 2,
            transcendentals=0,
        ),
    )(right_index, found, left_pick, right_flat)


def body(block_values, block_cols, live_count, out_pattern):
    depths = lax.axis_size("depth")
    columns = lax.axis_size("col")
    row_groups = lax.axis_size("row")
    row_index = lax.axis_index("row")
    rows_dev = block_values.shape[1]
    slot_count = block_values.shape[2]
    block_size = block_values.shape[3]
    group_rows = columns * rows_dev
    group_count = row_groups * depths
    total_rows = group_count * group_rows
    col_block = total_rows // columns
    pair_size = group_count // columns
    cap_left = slot_count // depths
    cap_right = pair_size * (slot_count // group_count) + min(pair_size, slot_count % group_count)
    values = block_values.reshape(rows_dev, slot_count, block_size, block_size)
    col_ids = block_cols.reshape(rows_dev, slot_count)
    counts = live_count.reshape(rows_dev)
    is_live = jnp.arange(slot_count, dtype=jnp.int32)[None, :] < counts[:, None]
    left_vals, left_cols = pack_slots(
        values, col_ids, col_ids // group_rows % depths, is_live, depths, cap_left
    )
    left_vals, left_cols = (
        lax.all_to_all(left_vals, "depth", split_axis=0, concat_axis=0, tiled=True),
        lax.all_to_all(left_cols, "depth", split_axis=0, concat_axis=0, tiled=True),
    )
    left_vals = lax.all_gather(left_vals[None], "col", axis=0, tiled=True)
    left_shape = left_cols.shape
    source_col = lax.broadcasted_iota(jnp.int32, left_shape, 0)
    source_depth = lax.broadcasted_iota(jnp.int32, left_shape, 1)
    source_row = lax.broadcasted_iota(jnp.int32, left_shape, 2)
    left_rows = (
        (row_index * depths + source_depth) * group_rows + source_col * rows_dev + source_row
    ).reshape(-1)
    left_flat = left_vals.reshape(-1, block_size, block_size)
    left_ids = left_cols.reshape(-1)
    right_vals, right_cols = pack_slots(
        values, col_ids, col_ids // col_block, is_live, columns, cap_right
    )
    right_vals = lax.all_to_all(right_vals, "col", split_axis=0, concat_axis=0, tiled=True)
    left_width = left_cols.size
    id_pack = jnp.concatenate(
        [
            jnp.broadcast_to(left_cols.reshape(1, -1), (columns, left_width)),
            right_cols.reshape(columns, -1),
        ],
        axis=1,
    )
    id_pack = lax.all_to_all(id_pack, "col", split_axis=0, concat_axis=0, tiled=True)
    left_cols = id_pack[:, :left_width].reshape((columns,) + left_cols.shape)
    right_cols = id_pack[:, left_width:].reshape(right_cols.shape)
    right_vals, right_cols = (
        lax.all_gather(right_vals[None], "row", axis=0, tiled=True),
        gather_by_exchange(right_cols, "row", row_groups),
    )
    right_flat = right_vals.reshape(-1, cap_right, block_size, block_size)
    right_ids = right_cols.reshape(-1, cap_right)
    pattern_rows = out_pattern[0, 0, :, 0]
    pattern_cols = out_pattern[0, 0, :, 1]
    local_row = pattern_rows - row_index * (depths * group_rows)
    left_pos = (local_row % group_rows) * depths + local_row // group_rows
    left_sel = left_pos[:, None] * cap_left + jnp.arange(cap_left, dtype=jnp.int32)[None, :]
    left_flat = left_vals.reshape(-1, block_size, block_size)
    left_ids = left_cols.reshape(-1)
    left_pick = jnp.take(left_flat, left_sel.reshape(-1), axis=0)
    inner = jnp.take(left_ids, left_sel, axis=0)
    safe_inner = jnp.maximum(inner, 0)
    right_row = safe_inner // (depths * group_rows) * columns + safe_inner % group_rows
    right_ids = right_cols.reshape(-1, cap_right)
    right_flat = right_vals.reshape(-1, block_size, block_size)
    right_here = jnp.take(right_ids, right_row, axis=0)
    matched = (right_here == pattern_cols[:, None, None]) & (inner >= 0)[:, :, None]
    slot = jnp.sum(
        jnp.where(matched, jnp.arange(cap_right, dtype=jnp.int32)[None, None, :], 0), axis=2
    )
    found = jnp.any(matched, axis=2)
    pattern_len = pattern_rows.shape[0]
    partial_sum = pair_products(
        (right_row * cap_right + slot).reshape(-1),
        found.reshape(-1).astype(jnp.int32),
        left_pick,
        right_flat,
    ).reshape(pattern_len, block_size, block_size)
    share = lax.psum_scatter(partial_sum[None, None], "depth", scatter_dimension=2, tiled=True)
    return jnp.log1p(share).astype(jnp.bfloat16)


def solution(mesh):
    in_specs = (
        P(("row", "depth"), "col", None, None, None),
        P(("row", "depth"), "col", None),
        P(("row", "depth"), "col"),
        P("row", "col", None, None),
    )
    out_specs = P("row", "col", "depth", None, None)
    return jax.shard_map(body, mesh=mesh, in_specs=in_specs, out_specs=out_specs, check_vma=False)
```

```python
import math

import jax
import jax.numpy as jnp
from jax import lax
from jax.experimental import pallas as pl
from jax.experimental.pallas import tpu as pltpu
from jax.sharding import PartitionSpec as P


def pack_slots(values, col_ids, targets, is_live, part_count, capacity):
    row_count = col_ids.shape[0]
    slot_count = col_ids.shape[1]
    block_size = values.shape[-1]
    chosen = (
        targets[:, :, None] == jnp.arange(part_count, dtype=jnp.int32)[None, None, :]
    ) & is_live[:, :, None]
    running = jnp.cumsum(chosen.astype(jnp.int32), axis=1) - 1
    picks = jnp.arange(capacity, dtype=jnp.int32)
    hit = jnp.transpose(chosen, (0, 2, 1))[:, :, None, :] & (
        jnp.transpose(running, (0, 2, 1))[:, :, None, :] == picks[None, None, :, None]
    )
    slot_ids = jnp.arange(slot_count, dtype=jnp.int32)
    source = jnp.sum(jnp.where(hit, slot_ids, 0), axis=3)
    filled = jnp.any(hit, axis=3)
    row_ids = jnp.arange(row_count, dtype=jnp.int32)[:, None, None]
    flat_source = (row_ids * slot_count + source).reshape(-1)
    blocks = jnp.take(values.reshape(-1, block_size, block_size), flat_source, axis=0)
    blocks = jnp.where(filled.reshape(-1)[:, None, None], blocks, jnp.zeros_like(blocks))
    cols = jnp.where(filled.reshape(-1), jnp.take(col_ids.reshape(-1), flat_source), -1)
    packed = blocks.reshape(row_count, part_count, capacity, block_size, block_size)
    packed_cols = cols.reshape(row_count, part_count, capacity)
    return (
        jnp.transpose(packed, (1, 0, 2, 3, 4)),
        jnp.transpose(packed_cols, (1, 0, 2)),
    )


def gather_by_exchange(x, axis, size):
    copies = jnp.broadcast_to(x[None], (size,) + x.shape)
    return lax.all_to_all(copies, axis, split_axis=0, concat_axis=0, tiled=True)


def pair_kernel(right_index, left_ref, right_hbm, out_ref, right_buf, sems):
    pairs, width, block_size = right_buf.shape
    per_pair = width // block_size
    copies = [
        pltpu.make_async_copy(
            right_hbm.at[right_index[t]],
            right_buf.at[t // per_pair, pl.ds((t % per_pair) * block_size, block_size)],
            sems.at[t],
        )
        for t in range(pairs * per_pair)
    ]
    for copy in copies:
        copy.start()
    for copy in copies:
        copy.wait()
    for p in range(pairs):
        out_ref[p] = jnp.dot(left_ref[p], right_buf[p], preferred_element_type=jnp.float32)


def pair_products(right_index, left_wide, right_flat):
    pairs, block_size, width = left_wide.shape
    return pl.pallas_call(
        pair_kernel,
        out_shape=jax.ShapeDtypeStruct((pairs, block_size, block_size), jnp.float32),
        in_specs=[
            pl.BlockSpec(memory_space=pltpu.SMEM),
            pl.BlockSpec(memory_space=pltpu.VMEM),
            pl.BlockSpec(memory_space=pl.ANY),
        ],
        out_specs=pl.BlockSpec(memory_space=pltpu.VMEM),
        scratch_shapes=[
            pltpu.VMEM((pairs, width, block_size), right_flat.dtype),
            pltpu.SemaphoreType.DMA((pairs * (width // block_size),)),
        ],
        cost_estimate=pl.CostEstimate(
            flops=2 * pairs * block_size * width * block_size,
            bytes_accessed=pairs * block_size * width * 2 * 2 + pairs * block_size * block_size * 4,
            transcendentals=0,
        ),
    )(right_index, left_wide, right_flat)


def body(block_values, block_cols, live_count, out_pattern):
    depths = lax.axis_size("depth")
    columns = lax.axis_size("col")
    row_groups = lax.axis_size("row")
    row_index = lax.axis_index("row")
    rows_dev = block_values.shape[1]
    slot_count = block_values.shape[2]
    block_size = block_values.shape[3]
    group_rows = columns * rows_dev
    group_count = row_groups * depths
    total_rows = group_count * group_rows
    col_block = total_rows // columns
    pair_size = group_count // columns
    cap_left = slot_count // depths
    cap_right = pair_size * (slot_count // group_count) + min(pair_size, slot_count % group_count)
    values = block_values.reshape(rows_dev, slot_count, block_size, block_size)
    col_ids = block_cols.reshape(rows_dev, slot_count)
    counts = live_count.reshape(rows_dev)
    is_live = jnp.arange(slot_count, dtype=jnp.int32)[None, :] < counts[:, None]
    left_vals, left_cols = pack_slots(
        values, col_ids, col_ids // group_rows % depths, is_live, depths, cap_left
    )
    left_vals, left_cols = (
        lax.all_to_all(left_vals, "depth", split_axis=0, concat_axis=0, tiled=True),
        lax.all_to_all(left_cols, "depth", split_axis=0, concat_axis=0, tiled=True),
    )
    left_vals = lax.all_gather(left_vals[None], "col", axis=0, tiled=True)
    left_shape = left_cols.shape
    source_col = lax.broadcasted_iota(jnp.int32, left_shape, 0)
    source_depth = lax.broadcasted_iota(jnp.int32, left_shape, 1)
    source_row = lax.broadcasted_iota(jnp.int32, left_shape, 2)
    left_rows = (
        (row_index * depths + source_depth) * group_rows + source_col * rows_dev + source_row
    ).reshape(-1)
    left_flat = left_vals.reshape(-1, block_size, block_size)
    left_ids = left_cols.reshape(-1)
    right_vals, right_cols = pack_slots(
        values, col_ids, col_ids // col_block, is_live, columns, cap_right
    )
    right_vals = lax.all_to_all(right_vals, "col", split_axis=0, concat_axis=0, tiled=True)
    left_width = left_cols.size
    id_pack = jnp.concatenate(
        [
            jnp.broadcast_to(left_cols.reshape(1, -1), (columns, left_width)),
            right_cols.reshape(columns, -1),
        ],
        axis=1,
    )
    id_pack = lax.all_to_all(id_pack, "col", split_axis=0, concat_axis=0, tiled=True)
    left_cols = id_pack[:, :left_width].reshape((columns,) + left_cols.shape)
    right_cols = id_pack[:, left_width:].reshape(right_cols.shape)
    right_vals, right_cols = (
        lax.all_gather(right_vals[None], "row", axis=0, tiled=True),
        gather_by_exchange(right_cols, "row", row_groups),
    )
    right_flat = right_vals.reshape(-1, cap_right, block_size, block_size)
    right_ids = right_cols.reshape(-1, cap_right)
    pattern_rows = out_pattern[0, 0, :, 0]
    pattern_cols = out_pattern[0, 0, :, 1]
    local_row = pattern_rows - row_index * (depths * group_rows)
    left_pos = (local_row % group_rows) * depths + local_row // group_rows
    left_sel = left_pos[:, None] * cap_left + jnp.arange(cap_left, dtype=jnp.int32)[None, :]
    left_flat = left_vals.reshape(-1, block_size, block_size)
    left_ids = left_cols.reshape(-1)
    left_pick = jnp.take(left_flat, left_sel.reshape(-1), axis=0)
    inner = jnp.take(left_ids, left_sel, axis=0)
    safe_inner = jnp.maximum(inner, 0)
    right_row = safe_inner // (depths * group_rows) * columns + safe_inner % group_rows
    right_ids = right_cols.reshape(-1, cap_right)
    right_flat = right_vals.reshape(-1, block_size, block_size)
    right_here = jnp.take(right_ids, right_row, axis=0)
    matched = (right_here == pattern_cols[:, None, None]) & (inner >= 0)[:, :, None]
    slot = jnp.sum(
        jnp.where(matched, jnp.arange(cap_right, dtype=jnp.int32)[None, None, :], 0), axis=2
    )
    found = jnp.any(matched, axis=2)
    pattern_len = pattern_rows.shape[0]
    left_wide = jnp.where(
        found.reshape(-1)[:, None, None], left_pick, jnp.zeros_like(left_pick)
    ).reshape(pattern_len, cap_left, block_size, block_size)
    left_wide = left_wide.transpose(0, 2, 1, 3).reshape(pattern_len, block_size, cap_left * block_size)
    partial_sum = pair_products(
        (right_row * cap_right + slot).reshape(-1), left_wide, right_flat
    )
    share = lax.psum_scatter(partial_sum[None, None], "depth", scatter_dimension=2, tiled=True)
    return jnp.log1p(share).astype(jnp.bfloat16)


def solution(mesh):
    in_specs = (
        P(("row", "depth"), "col", None, None, None),
        P(("row", "depth"), "col", None),
        P(("row", "depth"), "col"),
        P("row", "col", None, None),
    )
    out_specs = P("row", "col", "depth", None, None)
    return jax.shard_map(body, mesh=mesh, in_specs=in_specs, out_specs=out_specs, check_vma=False)
```

```python
import math

import jax
import jax.numpy as jnp
from jax import lax
from jax.experimental import pallas as pl
from jax.experimental.pallas import tpu as pltpu
from jax.sharding import PartitionSpec as P


def pack_slots(values, col_ids, targets, is_live, part_count, capacity):
    row_count = col_ids.shape[0]
    block_size = values.shape[-1]
    chosen = (
        targets[:, :, None] == jnp.arange(part_count, dtype=jnp.int32)[None, None, :]
    ) & is_live[:, :, None]
    running = jnp.cumsum(chosen.astype(jnp.int32), axis=1) - 1
    order_in = jnp.sum(jnp.where(chosen, running, 0), axis=2)
    row_ids = jnp.arange(row_count, dtype=jnp.int32)[:, None]
    total = part_count * row_count * capacity
    position = (targets * row_count + row_ids) * capacity + order_in
    position = jnp.where(is_live, position, total).reshape(-1)
    packed = jnp.zeros((total, block_size, block_size), values.dtype)
    packed = packed.at[position].set(values.reshape(-1, block_size, block_size), mode="drop")
    packed_cols = (
        jnp.full((total,), -1, jnp.int32).at[position].set(col_ids.reshape(-1), mode="drop")
    )
    return (
        packed.reshape(part_count, row_count, capacity, block_size, block_size),
        packed_cols.reshape(part_count, row_count, capacity),
    )


def gather_by_exchange(x, axis, size):
    copies = jnp.broadcast_to(x[None], (size,) + x.shape)
    return lax.all_to_all(copies, axis, split_axis=0, concat_axis=0, tiled=True)


def pair_kernel(right_index, found, left_ref, right_hbm, out_ref, right_buf, sems):
    count = right_buf.shape[0]
    copies = [
        pltpu.make_async_copy(right_hbm.at[right_index[t]], right_buf.at[t], sems.at[t])
        for t in range(count)
    ]
    for copy in copies:
        copy.start()
    for copy in copies:
        copy.wait()
    for p in range(count // 2):
        total = jnp.zeros(out_ref.shape[1:], jnp.float32)
        for t in (2 * p, 2 * p + 1):
            term = jnp.dot(left_ref[t], right_buf[t], preferred_element_type=jnp.float32)
            total = total + jnp.where(found[t] != 0, term, 0.0)
        out_ref[p] = total


def pair_products(right_index, found, left_pick, right_flat):
    count, block_size, _ = left_pick.shape
    return pl.pallas_call(
        pair_kernel,
        out_shape=jax.ShapeDtypeStruct((count // 2, block_size, block_size), jnp.float32),
        in_specs=[
            pl.BlockSpec(memory_space=pltpu.SMEM),
            pl.BlockSpec(memory_space=pltpu.SMEM),
            pl.BlockSpec(memory_space=pltpu.VMEM),
            pl.BlockSpec(memory_space=pl.ANY),
        ],
        out_specs=pl.BlockSpec(memory_space=pltpu.VMEM),
        scratch_shapes=[
            pltpu.VMEM((count, block_size, block_size), right_flat.dtype),
            pltpu.SemaphoreType.DMA((count,)),
        ],
        cost_estimate=pl.CostEstimate(
            flops=2 * count * block_size**3,
            bytes_accessed=count * block_size * block_size * 2 * 2 + count * block_size * block_size * 2,
            transcendentals=0,
        ),
    )(right_index, found, left_pick, right_flat)


def body(block_values, block_cols, live_count, out_pattern):
    depths = lax.axis_size("depth")
    columns = lax.axis_size("col")
    row_groups = lax.axis_size("row")
    row_index = lax.axis_index("row")
    rows_dev = block_values.shape[1]
    slot_count = block_values.shape[2]
    block_size = block_values.shape[3]
    group_rows = columns * rows_dev
    group_count = row_groups * depths
    total_rows = group_count * group_rows
    col_block = total_rows // columns
    pair_size = group_count // columns
    cap_left = slot_count // depths
    cap_right = pair_size * (slot_count // group_count) + min(pair_size, slot_count % group_count)
    values = block_values.reshape(rows_dev, slot_count, block_size, block_size)
    col_ids = block_cols.reshape(rows_dev, slot_count)
    counts = live_count.reshape(rows_dev)
    is_live = jnp.arange(slot_count, dtype=jnp.int32)[None, :] < counts[:, None]
    left_vals, left_cols = pack_slots(
        values, col_ids, col_ids // group_rows % depths, is_live, depths, cap_left
    )
    left_vals, left_cols = (
        lax.all_to_all(left_vals, "depth", split_axis=0, concat_axis=0, tiled=True),
        lax.all_to_all(left_cols, "depth", split_axis=0, concat_axis=0, tiled=True),
    )
    left_vals = lax.all_gather(left_vals[None], "col", axis=0, tiled=True)
    left_shape = left_cols.shape
    source_col = lax.broadcasted_iota(jnp.int32, left_shape, 0)
    source_depth = lax.broadcasted_iota(jnp.int32, left_shape, 1)
    source_row = lax.broadcasted_iota(jnp.int32, left_shape, 2)
    left_rows = (
        (row_index * depths + source_depth) * group_rows + source_col * rows_dev + source_row
    ).reshape(-1)
    left_flat = left_vals.reshape(-1, block_size, block_size)
    left_ids = left_cols.reshape(-1)
    values, left_vals = lax.optimization_barrier((values, left_vals))
    right_vals, right_cols = pack_slots(
        values, col_ids, col_ids // col_block, is_live, columns, cap_right
    )
    right_vals = lax.all_to_all(right_vals, "col", split_axis=0, concat_axis=0, tiled=True)
    left_width = left_cols.size
    id_pack = jnp.concatenate(
        [
            jnp.broadcast_to(left_cols.reshape(1, -1), (columns, left_width)),
            right_cols.reshape(columns, -1),
        ],
        axis=1,
    )
    id_pack = lax.all_to_all(id_pack, "col", split_axis=0, concat_axis=0, tiled=True)
    left_cols = id_pack[:, :left_width].reshape((columns,) + left_cols.shape)
    right_cols = id_pack[:, left_width:].reshape(right_cols.shape)
    right_vals, right_cols = (
        lax.all_gather(right_vals[None], "row", axis=0, tiled=True),
        gather_by_exchange(right_cols, "row", row_groups),
    )
    right_flat = right_vals.reshape(-1, cap_right, block_size, block_size)
    right_ids = right_cols.reshape(-1, cap_right)
    pattern_rows = out_pattern[0, 0, :, 0]
    pattern_cols = out_pattern[0, 0, :, 1]
    local_row = pattern_rows - row_index * (depths * group_rows)
    left_pos = (local_row % group_rows) * depths + local_row // group_rows
    left_sel = left_pos[:, None] * cap_left + jnp.arange(cap_left, dtype=jnp.int32)[None, :]
    left_flat = left_vals.reshape(-1, block_size, block_size)
    left_ids = left_cols.reshape(-1)
    left_pick = jnp.take(left_flat, left_sel.reshape(-1), axis=0)
    inner = jnp.take(left_ids, left_sel, axis=0)
    safe_inner = jnp.maximum(inner, 0)
    right_row = safe_inner // (depths * group_rows) * columns + safe_inner % group_rows
    right_ids = right_cols.reshape(-1, cap_right)
    right_flat = right_vals.reshape(-1, block_size, block_size)
    right_here = jnp.take(right_ids, right_row, axis=0)
    matched = (right_here == pattern_cols[:, None, None]) & (inner >= 0)[:, :, None]
    slot = jnp.sum(
        jnp.where(matched, jnp.arange(cap_right, dtype=jnp.int32)[None, None, :], 0), axis=2
    )
    found = jnp.any(matched, axis=2)
    pattern_len = pattern_rows.shape[0]
    partial_sum = pair_products(
        (right_row * cap_right + slot).reshape(-1),
        found.reshape(-1).astype(jnp.int32),
        left_pick,
        right_flat,
    ).reshape(pattern_len, block_size, block_size)
    share = lax.psum_scatter(partial_sum[None, None], "depth", scatter_dimension=2, tiled=True)
    return jnp.log1p(share).astype(jnp.bfloat16)


def solution(mesh):
    in_specs = (
        P(("row", "depth"), "col", None, None, None),
        P(("row", "depth"), "col", None),
        P(("row", "depth"), "col"),
        P("row", "col", None, None),
    )
    out_specs = P("row", "col", "depth", None, None)
    return jax.shard_map(body, mesh=mesh, in_specs=in_specs, out_specs=out_specs, check_vma=False)
```
